32 devices in a mesh: dimer: 4 (over y, x), grid: 8 (over z, core).
Axes of the slice: x: 2, y: 2, z: 4, core: 2. Of those that a mesh axis runs over, the one named last changes fastest.
Arguments:
- basis_values: bfloat16 [4, 10240, 1024], P('dimer', 'grid'), may hold values from -15 to 15
- aux_values: bfloat16 [4, 10240, 2048], P('dimer', 'grid'), may hold values from -6 to 6
- factors: bfloat16 [4, 512, 128], P('dimer', 'grid'), may hold values from -0.25 to 0.25
- frag_slot: int32 [4], replicated, may hold values from 0 to 3, each once
- dimer_pairs: int32 [4, 2], P('dimer'), may hold values from 0 to 3, as said below
- counts: int32 [4, 8], P('dimer', 'grid'), may hold values from 1 to 1280, 4096 in all within a row
- weights: float32 [4, 10240], P('dimer', 'grid'), may hold values from 0.00078125 to 0.003125
- metric_inv: float32 [4, 2048, 2048], P('dimer', 'grid'), may hold values from -1 to 1, as said below
Outputs:
- frag_fock: float32 [4, 512, 512], P('dimer', 'grid')
- coupling: float32 [4, 512, 512], P('dimer', 'grid')
The draws below stay inside these ranges and needn't reach their ends.
Inputs may be any that keep to these rules, and one draw needn't show every extreme that they name: `dimer_pairs`: each fragment is named by exactly two dimers, and the two fragments of a dimer differ. For each dimer the 8 counts sum to 4096 and the largest equals 1280. `metric_inv`: each matrix is symmetric.
All inputs are finite; a program needn't handle non-finite values. No bound on the sum of `counts` on one device may be relied on, other than what follows from the above.
Results may differ from the reference program's by a relative error of at most 0.0029.
Values may be sent and summed in bfloat16 or wider, within the bound.
No kernel may reach another device: no remote copies, remote signals or barrier semaphores. Data moves between devices by JAX's collectives and lax.ppermute only.
A program may use at most 64 MiB of HBM per device.

```python
import math
import jax
import jax.numpy as jnp
import numpy as np
from jax import lax

NB_F = 512
NOCC = 128
NAUX = 2048
PTS_DEV = 1280
NB = 1024
NDIMER = 4
NFRAG = 4
NPTS = 10240
LIVE = 4096
N_GRID = 8


def draw_dimer_pairs(key, part):
    order = jax.random.permutation(key, NFRAG).astype(jnp.int32)
    return jnp.stack([order, jnp.roll(order, -1)], axis=1)


def draw_basis_values(key, part):
    key_values, key_scale = jax.random.split(key)
    values = jax.random.truncated_normal(key_values, -5.0, 5.0, (NDIMER, NPTS, NB), jnp.float32)
    row_scale = jnp.exp(jax.random.uniform(key_scale, (NDIMER, NPTS, 1), jnp.float32, math.log(0.3), math.log(3.0)))
    return (values * row_scale).astype(jnp.bfloat16)


def draw_metric_inv(key, part):
    key_off, key_diag = jax.random.split(key)
    raw = jax.random.truncated_normal(key_off, -4.0, 4.0, (NDIMER, NAUX, NAUX), jnp.float32)
    symmetric = (raw + jnp.swapaxes(raw, 1, 2)) * (0.7 / NAUX)
    diagonal = jax.random.uniform(key_diag, (NDIMER, NAUX), jnp.float32, 2.0, 4.0)
    identity = jnp.eye(NAUX, dtype=jnp.float32)
    return symmetric + diagonal[:, :, None] * identity[None, :, :] * NAUX ** (-0.5)


def levels(stream_key, extent, cuts, least, high):
    level = 1.0
    for axis_at, blocks in cuts:
        heights = jax.random.uniform(jax.random.fold_in(jax.random.fold_in(stream_key, 6), axis_at), (blocks,), jnp.float32, least / len(cuts), high / len(cuts))
        level = level * jnp.repeat(jnp.exp(heights), extent[axis_at] // blocks).reshape((-1,) + (1,) * (len(extent) - 1 - axis_at))
    return level


def length_profile(amount, total, most, lean):
    loads = [(1 << 20) // math.isqrt(rank ** lean) + 1 for rank in range(2, amount + 1)]
    surplus, given = total - most - (amount - 1), [1] * (amount - 1)
    while surplus > 0:
        candidates = [i for i in range(amount - 1) if given[i] < most]
        mass, left = sum([loads[i] for i in candidates]), surplus
        for i in candidates:
            addition = min(most - given[i], max(1, left * loads[i] // mass), surplus)
            given[i] = given[i] + addition
            surplus = surplus - addition
    return np.array([most] + given)


def uneven_parts(stream_key, count, total, bound, slope):
    if count == 2:
        one = jax.random.randint(stream_key, (), max(1, total - bound), min(bound, total - 1) + 1)
        return jnp.stack([one, total - one])
    lengths = jnp.asarray(length_profile(count, total, bound, slope), jnp.int32)
    couples = (count - 1) // 2
    source_of, receiver = lengths[1:1 + 2 * couples:2], lengths[2:2 + 2 * couples:2]
    room = jnp.minimum(source_of - 1, bound - receiver)
    shifted = jax.random.randint(jax.random.fold_in(stream_key, 1), (couples,), 0, 1 << 20) % (room + 1)
    lengths = lengths.at[1:1 + 2 * couples:2].set(source_of - shifted).at[2:2 + 2 * couples:2].set(receiver + shifted)
    return lengths[jax.random.permutation(jax.random.fold_in(stream_key, 2), count)]


def bell_draw(rng, shape, scale, bound, shards=(), kind=jnp.bfloat16):
    factor_of = levels(rng, shape, shards, -0.22, 0.18) if shards else 1.0
    entries = jax.random.normal(rng, shape, jnp.float32) * scale * factor_of
    return jnp.minimum(jnp.maximum(entries, -bound), bound).astype(kind)


def setup_inputs(seed: int = 0) -> dict:
    splits = jax.random.split(jax.random.key(seed), 9)
    return {
        "basis_values": draw_basis_values(jax.random.fold_in(splits[8], 71), 0),
        "aux_values": bell_draw(splits[1], (NDIMER, NPTS, NAUX), 1.0, 6.0, ((0, 4), (1, 8))),
        "factors": bell_draw(splits[2], (NFRAG, NB_F, NOCC), NB_F ** -0.5, 0.25, ((0, 4), (1, 8))),
        "frag_slot": jax.random.permutation(splits[3], NFRAG).astype(jnp.int32),
        "dimer_pairs": draw_dimer_pairs(jax.random.fold_in(splits[8], 71), 0),
        "counts": jax.vmap(lambda own: uneven_parts(own, N_GRID, LIVE, PTS_DEV, 2))(jax.random.split(splits[5], NDIMER)).reshape((NDIMER, N_GRID)).astype(jnp.int32),
        "weights": jnp.clip(jnp.exp(math.log(0.003125) - 1.3862944 * jax.random.uniform(splits[6], (NDIMER, NPTS), jnp.float32) ** levels(splits[6], (NDIMER, NPTS), ((0, 4), (1, 8)), -0.2, 0.2)), 0.00078125, 0.003125),
        "metric_inv": draw_metric_inv(jax.random.fold_in(splits[8], 71), 0),
    }


exchange_coeff = 0.9847450218426964


def reference(basis_values, aux_values, factors, frag_slot, dimer_pairs, counts, weights, metric_inv):
    highest = lax.Precision.HIGHEST
    frag_fock = jnp.zeros((NFRAG, NB_F, NB_F), jnp.float32)
    couplings = []
    position = jnp.arange(NPTS, dtype=jnp.int32)
    owner_device = position // PTS_DEV
    offset = position % PTS_DEV
    for dimer_index in range(NDIMER):
        basis_rows = basis_values[dimer_index]
        aux_float = aux_values[dimer_index].astype(jnp.float32)
        live_weight = jnp.where(offset < counts[dimer_index][owner_device], weights[dimer_index], jnp.zeros((), jnp.float32))
        first_factor = factors[frag_slot[dimer_pairs[dimer_index, 0]]]
        second_factor = factors[frag_slot[dimer_pairs[dimer_index, 1]]]
        orb_first = jnp.dot(basis_rows[:, :NB_F], first_factor, preferred_element_type=jnp.float32)
        orb_second = jnp.dot(basis_rows[:, NB_F:], second_factor, preferred_element_type=jnp.float32)
        density = (jnp.sum(orb_first * orb_first, axis=1) + jnp.sum(orb_second * orb_second, axis=1)) / (2.0 * NOCC)
        exchange = -exchange_coeff * jnp.cbrt(density)
        fitted = jnp.dot(live_weight * density, aux_float, precision=highest)
        coefficients = jnp.dot(metric_inv[dimer_index], fitted, precision=highest)
        coulomb = jnp.dot(aux_float, coefficients, precision=highest)
        average = jnp.sum(live_weight * (coulomb + exchange)) / jnp.sum(live_weight)
        potential = live_weight * (coulomb + exchange - average)
        weighted_basis = (basis_rows * potential[:, None]).astype(jnp.bfloat16)
        dimer_fock = lax.dot_general(weighted_basis, basis_rows, (((0,), (0,)), ((), ())), preferred_element_type=jnp.float32)
        frag_fock = frag_fock.at[dimer_pairs[dimer_index, 0]].add(dimer_fock[:NB_F, :NB_F])
        frag_fock = frag_fock.at[dimer_pairs[dimer_index, 1]].add(dimer_fock[NB_F:, NB_F:])
        couplings.append(dimer_fock[:NB_F, NB_F:])
    return frag_fock, jnp.stack(couplings)
```

```python
import jax
import jax.numpy as jnp
from jax import lax
from jax.sharding import PartitionSpec as P

exchange_coeff = 0.9847450218426964


def split_rows(rows):
    high_part = rows.astype(jnp.bfloat16)
    high_back = lax.optimization_barrier(high_part).astype(jnp.float32)
    low_part = (rows - high_back).astype(jnp.bfloat16)
    return high_part, low_part


def contract(left_side, right_side):
    numbers = (((0,), (0,)), ((), ()))
    return lax.dot_general(left_side, right_side, numbers, preferred_element_type=jnp.float32)


def shards(basis_values, aux_values, factors, frag_slot, dimer_pairs, counts, weights, metric_inv):
    highest = lax.Precision.HIGHEST
    basis_rows = basis_values[0]
    aux_block = aux_values[0]
    points = basis_rows.shape[0]
    naux = aux_block.shape[1]
    frag_basis = basis_rows.shape[1] // 2
    live_count = counts[0, 0]
    position = lax.iota(jnp.int32, points)
    live_weight = jnp.where(position < live_count, weights[0], jnp.zeros((), jnp.float32))
    gathered = lax.all_gather(factors, "dimer", axis=0, tiled=True)
    frag_ids = lax.iota(jnp.int32, frag_slot.shape[0])
    wanted = jnp.sum(
        jnp.where(frag_ids[None, :] == dimer_pairs[0][:, None], frag_slot[None, :], 0), axis=1
    )
    selector = (frag_ids[None, :] == wanted[:, None]).astype(jnp.bfloat16)
    chosen = jnp.einsum(
        "as,srk->ark", selector, gathered, preferred_element_type=jnp.float32
    ).astype(jnp.bfloat16)
    dimer_factors = lax.all_gather(chosen, "grid", axis=1, tiled=True)
    orb_first = jnp.dot(
        basis_rows[:, :frag_basis], dimer_factors[0], preferred_element_type=jnp.float32
    )
    orb_second = jnp.dot(
        basis_rows[:, frag_basis:], dimer_factors[1], preferred_element_type=jnp.float32
    )
    density = (
        jnp.sum(orb_first * orb_first, axis=1) + jnp.sum(orb_second * orb_second, axis=1)
    ) / (2.0 * dimer_factors.shape[2])
    exchange = -exchange_coeff * jnp.cbrt(density)
    weighted_density = live_weight * density
    high_rows, low_rows = split_rows(jnp.stack([weighted_density, live_weight]))
    projections = jnp.dot(
        jnp.concatenate([high_rows, low_rows]), aux_block, preferred_element_type=jnp.float32
    )
    fitted_part = projections[0] + projections[2]
    weight_part = projections[1] + projections[3]
    sums_part = jnp.stack([jnp.sum(live_weight * exchange), jnp.sum(live_weight)])
    payload = jnp.concatenate([fitted_part, weight_part, sums_part])
    totals = lax.psum(payload, "grid")
    fitted = totals[:naux]
    weight_projection = totals[naux : 2 * naux]
    exchange_total = totals[2 * naux]
    weight_sum = totals[2 * naux + 1]
    coef_rows = jnp.dot(metric_inv[0], fitted, precision=highest)
    coefficients = lax.all_gather(coef_rows, "grid", axis=0, tiled=True)
    coef_high, coef_low = split_rows(coefficients)
    coulomb_parts = jnp.dot(
        aux_block, jnp.stack([coef_high, coef_low], axis=1), preferred_element_type=jnp.float32
    )
    coulomb = coulomb_parts[:, 0] + coulomb_parts[:, 1]
    potential_total = jnp.dot(coefficients, weight_projection, precision=highest) + exchange_total
    average = potential_total / weight_sum
    potential = live_weight * (coulomb + exchange - average)
    weighted_basis = (basis_rows * potential[:, None]).astype(jnp.bfloat16)
    half_rows = frag_basis // lax.axis_size("grid")
    left_first = lax.slice_in_dim(weighted_basis, 0, half_rows * lax.axis_size("grid"), axis=1)
    left_second = lax.dynamic_slice_in_dim(
        weighted_basis, frag_basis, half_rows * lax.axis_size("grid"), 1
    )
    first_first = contract(left_first, basis_rows[:, :frag_basis])
    first_second = contract(left_first, basis_rows[:, frag_basis:])
    second_second = contract(left_second, basis_rows[:, frag_basis:])
    shares = lax.psum_scatter(
        jnp.stack([first_first, first_second, second_second], axis=1),
        "grid",
        scatter_dimension=0,
        tiled=True,
    )
    own_first = shares[:, 0]
    own_cross = shares[:, 1]
    own_second = shares[:, 2]
    groups = lax.axis_size("dimer")
    me = lax.axis_index("dimer")
    zero = jnp.zeros((), jnp.float32)

    def piece(dest):
        return jnp.where(dimer_pairs[0, 0] == dest, own_first, zero) + jnp.where(
            dimer_pairs[0, 1] == dest, own_second, zero
        )

    frag_fock = piece(me)
    for shift in range(1, groups):
        sent = piece(lax.rem(me + shift, groups))
        frag_fock = frag_fock + lax.ppermute(
            sent, "dimer", [(i, (i + shift) % groups) for i in range(groups)]
        )
    return (frag_fock[None], own_cross[None])


def solution(mesh):
    placed = (
        P("dimer", "grid", None),
        P("dimer", "grid", None),
        P("dimer", "grid", None),
        P(),
        P("dimer", None),
        P("dimer", "grid"),
        P("dimer", "grid"),
        P("dimer", "grid", None),
    )
    return jax.shard_map(
        shards,
        mesh=mesh,
        in_specs=placed,
        out_specs=(P("dimer", "grid", None), P("dimer", "grid", None)),
        check_vma=False,
    )
```

```python
import jax
import jax.numpy as jnp
from jax import lax
from jax.sharding import PartitionSpec as P

exchange_coeff = 0.9847450218426964


def split_rows(rows):
    high_part = rows.astype(jnp.bfloat16)
    high_back = lax.optimization_barrier(high_part).astype(jnp.float32)
    low_part = (rows - high_back).astype(jnp.bfloat16)
    return high_part, low_part


def contract(left_side, right_side):
    numbers = (((0,), (0,)), ((), ()))
    return lax.dot_general(left_side, right_side, numbers, preferred_element_type=jnp.float32)


def xor_sum(value, axis):
    size = lax.axis_size(axis)
    if size & (size - 1):
        return lax.psum(value, axis)
    step = 1
    while step < size:
        value = value + lax.ppermute(value, axis, [(i, i ^ step) for i in range(size)])
        step *= 2
    return value


def xor_gather(value, axis, dim):
    size = lax.axis_size(axis)
    if size & (size - 1):
        return lax.all_gather(value, axis, axis=dim, tiled=True)
    me = lax.axis_index(axis)
    step = 1
    while step < size:
        other = lax.ppermute(value, axis, [(i, i ^ step) for i in range(size)])
        value = jnp.where(
            (me & step) == 0,
            jnp.concatenate([value, other], axis=dim),
            jnp.concatenate([other, value], axis=dim),
        )
        step *= 2
    return value


def shards(basis_values, aux_values, factors, frag_slot, dimer_pairs, counts, weights, metric_inv):
    highest = lax.Precision.HIGHEST
    basis_rows = basis_values[0]
    aux_block = aux_values[0]
    points = basis_rows.shape[0]
    naux = aux_block.shape[1]
    frag_basis = basis_rows.shape[1] // 2
    live_count = counts[0, 0]
    position = lax.iota(jnp.int32, points)
    live_weight = jnp.where(position < live_count, weights[0], jnp.zeros((), jnp.float32))
    gathered = xor_gather(factors, "dimer", 0)
    frag_ids = lax.iota(jnp.int32, frag_slot.shape[0])
    wanted = jnp.sum(
        jnp.where(frag_ids[None, :] == dimer_pairs[0][:, None], frag_slot[None, :], 0), axis=1
    )
    selector = (frag_ids[None, :] == wanted[:, None]).astype(jnp.bfloat16)
    chosen = jnp.einsum(
        "as,srk->ark", selector, gathered, preferred_element_type=jnp.float32
    ).astype(jnp.bfloat16)
    dimer_factors = xor_gather(chosen, "grid", 1)
    orb_first = jnp.dot(
        basis_rows[:, :frag_basis], dimer_factors[0], preferred_element_type=jnp.float32
    )
    orb_second = jnp.dot(
        basis_rows[:, frag_basis:], dimer_factors[1], preferred_element_type=jnp.float32
    )
    density = (
        jnp.sum(orb_first * orb_first, axis=1) + jnp.sum(orb_second * orb_second, axis=1)
    ) / (2.0 * dimer_factors.shape[2])
    exchange = -exchange_coeff * jnp.cbrt(density)
    weighted_density = live_weight * density
    high_rows, low_rows = split_rows(jnp.stack([weighted_density, live_weight]))
    projections = jnp.dot(
        jnp.concatenate([high_rows, low_rows]), aux_block, preferred_element_type=jnp.float32
    )
    fitted_part = projections[0] + projections[2]
    weight_part = projections[1] + projections[3]
    sums_part = jnp.stack([jnp.sum(live_weight * exchange), jnp.sum(live_weight)])
    payload = jnp.concatenate([fitted_part, weight_part, sums_part])
    totals = xor_sum(payload, "grid")
    fitted = totals[:naux]
    weight_projection = totals[naux : 2 * naux]
    exchange_total = totals[2 * naux]
    weight_sum = totals[2 * naux + 1]
    coef_rows = jnp.dot(metric_inv[0], fitted, precision=highest)
    coefficients = lax.all_gather(coef_rows, "grid", axis=0, tiled=True)
    coef_high, coef_low = split_rows(coefficients)
    coulomb_parts = jnp.dot(
        aux_block, jnp.stack([coef_high, coef_low], axis=1), preferred_element_type=jnp.float32
    )
    coulomb = coulomb_parts[:, 0] + coulomb_parts[:, 1]
    potential_total = jnp.dot(coefficients, weight_projection, precision=highest) + exchange_total
    average = potential_total / weight_sum
    potential = live_weight * (coulomb + exchange - average)
    weighted_basis = (basis_rows * potential[:, None]).astype(jnp.bfloat16)
    half_rows = frag_basis // lax.axis_size("grid")
    left_first = lax.slice_in_dim(weighted_basis, 0, half_rows * lax.axis_size("grid"), axis=1)
    left_second = lax.dynamic_slice_in_dim(
        weighted_basis, frag_basis, half_rows * lax.axis_size("grid"), 1
    )
    first_first = contract(left_first, basis_rows[:, :frag_basis])
    first_second = contract(left_first, basis_rows[:, frag_basis:])
    second_second = contract(left_second, basis_rows[:, frag_basis:])
    shares = lax.psum_scatter(
        jnp.stack([first_first, first_second, second_second], axis=1),
        "grid",
        scatter_dimension=0,
        tiled=True,
    )
    own_first = shares[:, 0]
    own_cross = shares[:, 1]
    own_second = shares[:, 2]
    groups = lax.axis_size("dimer")
    me = lax.axis_index("dimer")
    zero = jnp.zeros((), jnp.float32)

    def piece(dest):
        return jnp.where(dimer_pairs[0, 0] == dest, own_first, zero) + jnp.where(
            dimer_pairs[0, 1] == dest, own_second, zero
        )

    frag_fock = piece(me)
    for shift in range(1, groups):
        sent = piece(lax.rem(me + shift, groups))
        frag_fock = frag_fock + lax.ppermute(
            sent, "dimer", [(i, (i + shift) % groups) for i in range(groups)]
        )
    return (frag_fock[None], own_cross[None])


def solution(mesh):
    placed = (
        P("dimer", "grid", None),
        P("dimer", "grid", None),
        P("dimer", "grid", None),
        P(),
        P("dimer", None),
        P("dimer", "grid"),
        P("dimer", "grid"),
        P("dimer", "grid", None),
    )
    return jax.shard_map(
        shards,
        mesh=mesh,
        in_specs=placed,
        out_specs=(P("dimer", "grid", None), P("dimer", "grid", None)),
        check_vma=False,
    )
```

```python
import jax
import jax.numpy as jnp
from jax import lax
from jax.sharding import PartitionSpec as P

exchange_coeff = 0.9847450218426964


def split_rows(rows):
    high_part = rows.astype(jnp.bfloat16)
    high_back = lax.optimization_barrier(high_part).astype(jnp.float32)
    low_part = (rows - high_back).astype(jnp.bfloat16)
    return high_part, low_part


def contract(left_side, right_side):
    numbers = (((0,), (0,)), ((), ()))
    return lax.dot_general(left_side, right_side, numbers, preferred_element_type=jnp.float32)


def xor_sum(value, axis):
    size = lax.axis_size(axis)
    if size & (size - 1):
        return lax.psum(value, axis)
    step = 1
    while step < size:
        value = value + lax.ppermute(value, axis, [(i, i ^ step) for i in range(size)])
        step *= 2
    return value


def xor_gather(value, axis, dim):
    size = lax.axis_size(axis)
    if size & (size - 1):
        return lax.all_gather(value, axis, axis=dim, tiled=True)
    me = lax.axis_index(axis)
    step = 1
    while step < size:
        other = lax.ppermute(value, axis, [(i, i ^ step) for i in range(size)])
        value = jnp.where(
            (me & step) == 0,
            jnp.concatenate([value, other], axis=dim),
            jnp.concatenate([other, value], axis=dim),
        )
        step *= 2
    return value


def shards(basis_values, aux_values, factors, frag_slot, dimer_pairs, counts, weights, metric_inv):
    highest = lax.Precision.HIGHEST
    basis_rows = basis_values[0]
    aux_block = aux_values[0]
    points = basis_rows.shape[0]
    naux = aux_block.shape[1]
    frag_basis = basis_rows.shape[1] // 2
    live_count = counts[0, 0]
    position = lax.iota(jnp.int32, points)
    live_weight = jnp.where(position < live_count, weights[0], jnp.zeros((), jnp.float32))
    gathered = xor_gather(factors, "dimer", 0)
    frag_ids = lax.iota(jnp.int32, frag_slot.shape[0])
    wanted = jnp.sum(
        jnp.where(frag_ids[None, :] == dimer_pairs[0][:, None], frag_slot[None, :], 0), axis=1
    )
    selector = (frag_ids[None, :] == wanted[:, None]).astype(jnp.bfloat16)
    chosen = jnp.einsum(
        "as,srk->ark", selector, gathered, preferred_element_type=jnp.float32
    ).astype(jnp.bfloat16)
    dimer_factors = xor_gather(chosen, "grid", 1)
    orb_first = jnp.dot(
        basis_rows[:, :frag_basis], dimer_factors[0], preferred_element_type=jnp.float32
    )
    orb_second = jnp.dot(
        basis_rows[:, frag_basis:], dimer_factors[1], preferred_element_type=jnp.float32
    )
    density = (
        jnp.sum(orb_first * orb_first, axis=1) + jnp.sum(orb_second * orb_second, axis=1)
    ) / (2.0 * dimer_factors.shape[2])
    exchange = -exchange_coeff * jnp.cbrt(density)
    weighted_density = live_weight * density
    high_rows, low_rows = split_rows(jnp.stack([weighted_density, live_weight]))
    projections = jnp.dot(
        jnp.concatenate([high_rows, low_rows]), aux_block, preferred_element_type=jnp.float32
    )
    fitted_part = projections[0] + projections[2]
    weight_part = projections[1] + projections[3]
    sums_part = jnp.stack([jnp.sum(live_weight * exchange), jnp.sum(live_weight)])
    payload = jnp.concatenate([fitted_part, weight_part, sums_part])
    totals = xor_sum(payload, "grid")
    fitted = totals[:naux]
    weight_projection = totals[naux : 2 * naux]
    exchange_total = totals[2 * naux]
    weight_sum = totals[2 * naux + 1]
    coef_rows = jnp.dot(metric_inv[0], fitted, precision=highest)
    coefficients = xor_gather(coef_rows, "grid", 0)
    coef_high, coef_low = split_rows(coefficients)
    coulomb_parts = lax.dot_general(
        jnp.stack([coef_high, coef_low]),
        aux_block,
        (((1,), (1,)), ((), ())),
        preferred_element_type=jnp.float32,
    )
    coulomb = coulomb_parts[0] + coulomb_parts[1]
    potential_total = jnp.dot(coefficients, weight_projection, precision=highest) + exchange_total
    average = potential_total / weight_sum
    potential = live_weight * (coulomb + exchange - average)
    weighted_basis = (basis_rows * potential[:, None]).astype(jnp.bfloat16)
    half_rows = frag_basis // lax.axis_size("grid")
    left_first = lax.slice_in_dim(weighted_basis, 0, half_rows * lax.axis_size("grid"), axis=1)
    left_second = lax.dynamic_slice_in_dim(
        weighted_basis, frag_basis, half_rows * lax.axis_size("grid"), 1
    )
    first_first = contract(left_first, basis_rows[:, :frag_basis])
    first_second = contract(left_first, basis_rows[:, frag_basis:])
    second_second = contract(left_second, basis_rows[:, frag_basis:])
    diagonal = lax.psum_scatter(
        jnp.stack([first_first, second_second], axis=1), "grid", scatter_dimension=0, tiled=True
    )
    own_cross = lax.psum_scatter(first_second, "grid", scatter_dimension=0, tiled=True)
    own_first = diagonal[:, 0]
    own_second = diagonal[:, 1]
    groups = lax.axis_size("dimer")
    me = lax.axis_index("dimer")
    zero = jnp.zeros((), jnp.float32)

    def piece(dest):
        return jnp.where(dimer_pairs[0, 0] == dest, own_first, zero) + jnp.where(
            dimer_pairs[0, 1] == dest, own_second, zero
        )

    frag_fock = piece(me)
    for shift in range(1, groups):
        sent = piece(lax.rem(me + shift, groups))
        frag_fock = frag_fock + lax.ppermute(
            sent, "dimer", [(i, (i + shift) % groups) for i in range(groups)]
        )
    return (frag_fock[None], own_cross[None])


def solution(mesh):
    placed = (
        P("dimer", "grid", None),
        P("dimer", "grid", None),
        P("dimer", "grid", None),
        P(),
        P("dimer", None),
        P("dimer", "grid"),
        P("dimer", "grid"),
        P("dimer", "grid", None),
    )
    return jax.shard_map(
        shards,
        mesh=mesh,
        in_specs=placed,
        out_specs=(P("dimer", "grid", None), P("dimer", "grid", None)),
        check_vma=False,
    )
```

```python
import jax
import jax.numpy as jnp
from jax import lax
from jax.sharding import PartitionSpec as P

exchange_coeff = 0.9847450218426964


def split_rows(rows):
    high_part = rows.astype(jnp.bfloat16)
    high_back = lax.optimization_barrier(high_part).astype(jnp.float32)
    low_part = (rows - high_back).astype(jnp.bfloat16)
    return high_part, low_part


def contract(left_side, right_side):
    numbers = (((0,), (0,)), ((), ()))
    return lax.dot_general(left_side, right_side, numbers, preferred_element_type=jnp.float32)


def xor_sum(value, axis):
    size = lax.axis_size(axis)
    if size & (size - 1):
        return lax.psum(value, axis)
    step = 1
    while step < size:
        value = value + lax.ppermute(value, axis, [(i, i ^ step) for i in range(size)])
        step *= 2
    return value


def xor_gather(value, axis, dim):
    size = lax.axis_size(axis)
    if size & (size - 1):
        return lax.all_gather(value, axis, axis=dim, tiled=True)
    me = lax.axis_index(axis)
    step = 1
    while step < size:
        other = lax.ppermute(value, axis, [(i, i ^ step) for i in range(size)])
        value = jnp.where(
            (me & step) == 0,
            jnp.concatenate([value, other], axis=dim),
            jnp.concatenate([other, value], axis=dim),
        )
        step *= 2
    return value


def xor_scatter(value, axis):
    size = lax.axis_size(axis)
    if size & (size - 1):
        return lax.psum_scatter(value, axis, scatter_dimension=0, tiled=True)
    me = lax.axis_index(axis)
    value = value.reshape((size, value.shape[0] // size) + value.shape[1:])
    bit = 0
    while (1 << bit) < size:
        pairs = value.reshape((value.shape[0] // 2, 2) + value.shape[1:])
        mine = (me >> bit) & 1
        keep = lax.dynamic_index_in_dim(pairs, mine, axis=1, keepdims=False)
        send = lax.dynamic_index_in_dim(pairs, 1 - mine, axis=1, keepdims=False)
        value = keep + lax.ppermute(send, axis, [(i, i ^ (1 << bit)) for i in range(size)])
        bit += 1
    return value[0]


def shards(basis_values, aux_values, factors, frag_slot, dimer_pairs, counts, weights, metric_inv):
    highest = lax.Precision.HIGHEST
    basis_rows = basis_values[0]
    aux_block = aux_values[0]
    points = basis_rows.shape[0]
    naux = aux_block.shape[1]
    frag_basis = basis_rows.shape[1] // 2
    live_count = counts[0, 0]
    position = lax.iota(jnp.int32, points)
    live_weight = jnp.where(position < live_count, weights[0], jnp.zeros((), jnp.float32))
    gathered = xor_gather(factors, "dimer", 0)
    frag_ids = lax.iota(jnp.int32, frag_slot.shape[0])
    wanted = jnp.sum(
        jnp.where(frag_ids[None, :] == dimer_pairs[0][:, None], frag_slot[None, :], 0), axis=1
    )
    selector = (frag_ids[None, :] == wanted[:, None]).astype(jnp.bfloat16)
    chosen = jnp.einsum(
        "as,srk->ark", selector, gathered, preferred_element_type=jnp.float32
    ).astype(jnp.bfloat16)
    dimer_factors = xor_gather(chosen, "grid", 1)
    orb_first = jnp.dot(
        basis_rows[:, :frag_basis], dimer_factors[0], preferred_element_type=jnp.float32
    )
    orb_second = jnp.dot(
        basis_rows[:, frag_basis:], dimer_factors[1], preferred_element_type=jnp.float32
    )
    density = (
        jnp.sum(orb_first * orb_first, axis=1) + jnp.sum(orb_second * orb_second, axis=1)
    ) / (2.0 * dimer_factors.shape[2])
    exchange = -exchange_coeff * jnp.cbrt(density)
    weighted_density = live_weight * density
    high_rows, low_rows = split_rows(jnp.stack([weighted_density, live_weight]))
    projections = jnp.dot(
        jnp.concatenate([high_rows, low_rows]), aux_block, preferred_element_type=jnp.float32
    )
    fitted_part = projections[0] + projections[2]
    weight_part = projections[1] + projections[3]
    sums_part = jnp.stack([jnp.sum(live_weight * exchange), jnp.sum(live_weight)])
    payload = jnp.concatenate([fitted_part, weight_part, sums_part])
    totals = xor_sum(payload, "grid")
    fitted = totals[:naux]
    weight_projection = totals[naux : 2 * naux]
    exchange_total = totals[2 * naux]
    weight_sum = totals[2 * naux + 1]
    coef_rows = jnp.dot(metric_inv[0], fitted, precision=highest)
    coefficients = xor_gather(coef_rows, "grid", 0)
    coef_high, coef_low = split_rows(coefficients)
    coulomb_parts = jnp.dot(
        aux_block, jnp.stack([coef_high, coef_low], axis=1), preferred_element_type=jnp.float32
    )
    coulomb = coulomb_parts[:, 0] + coulomb_parts[:, 1]
    potential_total = jnp.dot(coefficients, weight_projection, precision=highest) + exchange_total
    average = potential_total / weight_sum
    potential = live_weight * (coulomb + exchange - average)
    weighted_basis = (basis_rows * potential[:, None]).astype(jnp.bfloat16)
    half_rows = frag_basis // lax.axis_size("grid")
    left_first = lax.slice_in_dim(weighted_basis, 0, half_rows * lax.axis_size("grid"), axis=1)
    left_second = lax.dynamic_slice_in_dim(
        weighted_basis, frag_basis, half_rows * lax.axis_size("grid"), 1
    )
    first_first = contract(left_first, basis_rows[:, :frag_basis])
    first_second = contract(left_first, basis_rows[:, frag_basis:])
    second_second = contract(left_second, basis_rows[:, frag_basis:])
    shares = xor_scatter(jnp.stack([first_first, first_second, second_second], axis=1), "grid")
    own_first = shares[:, 0]
    own_cross = shares[:, 1]
    own_second = shares[:, 2]
    groups = lax.axis_size("dimer")
    me = lax.axis_index("dimer")
    zero = jnp.zeros((), jnp.float32)

    def piece(dest):
        return jnp.where(dimer_pairs[0, 0] == dest, own_first, zero) + jnp.where(
            dimer_pairs[0, 1] == dest, own_second, zero
        )

    frag_fock = piece(me)
    for shift in range(1, groups):
        sent = piece(lax.rem(me + shift, groups))
        frag_fock = frag_fock + lax.ppermute(
            sent, "dimer", [(i, (i + shift) % groups) for i in range(groups)]
        )
    return (frag_fock[None], own_cross[None])


def solution(mesh):
    placed = (
        P("dimer", "grid", None),
        P("dimer", "grid", None),
        P("dimer", "grid", None),
        P(),
        P("dimer", None),
        P("dimer", "grid"),
        P("dimer", "grid"),
        P("dimer", "grid", None),
    )
    return jax.shard_map(
        shards,
        mesh=mesh,
        in_specs=placed,
        out_specs=(P("dimer", "grid", None), P("dimer", "grid", None)),
        check_vma=False,
    )
```

```python
import jax
import jax.numpy as jnp
from jax import lax
from jax.sharding import PartitionSpec as P

exchange_coeff = 0.9847450218426964


def split_rows(rows):
    high_part = rows.astype(jnp.bfloat16)
    high_back = lax.optimization_barrier(high_part).astype(jnp.float32)
    low_part = (rows - high_back).astype(jnp.bfloat16)
    return high_part, low_part


def contract(left_side, right_side):
    numbers = (((0,), (0,)), ((), ()))
    return lax.dot_general(left_side, right_side, numbers, preferred_element_type=jnp.float32)


def xor_sum(value, axis):
    size = lax.axis_size(axis)
    if size & (size - 1):
        return lax.psum(value, axis)
    step = 1
    while step < size:
        value = value + lax.ppermute(value, axis, [(i, i ^ step) for i in range(size)])
        step *= 2
    return value


def xor_gather(value, axis, dim):
    size = lax.axis_size(axis)
    if size & (size - 1):
        return lax.all_gather(value, axis, axis=dim, tiled=True)
    me = lax.axis_index(axis)
    step = 1
    while step < size:
        other = lax.ppermute(value, axis, [(i, i ^ step) for i in range(size)])
        value = jnp.where(
            (me & step) == 0,
            jnp.concatenate([value, other], axis=dim),
            jnp.concatenate([other, value], axis=dim),
        )
        step *= 2
    return value


def scatter_chunks(value, axis):
    size = lax.axis_size(axis)
    return value.reshape((size, value.shape[0] // size) + value.shape[1:])


def scatter_step(value, axis, bit):
    size = lax.axis_size(axis)
    mine = (lax.axis_index(axis) >> bit) & 1
    pairs = value.reshape((value.shape[0] // 2, 2) + value.shape[1:])
    keep = lax.dynamic_index_in_dim(pairs, mine, axis=1, keepdims=False)
    send = lax.dynamic_index_in_dim(pairs, 1 - mine, axis=1, keepdims=False)
    return keep + lax.ppermute(send, axis, [(i, i ^ (1 << bit)) for i in range(size)])


def paired_scatter(lead, follow, axis):
    size = lax.axis_size(axis)
    if size & (size - 1):
        return (
            lax.psum_scatter(lead, axis, scatter_dimension=0, tiled=True),
            lax.psum_scatter(follow, axis, scatter_dimension=0, tiled=True),
        )
    lead = scatter_chunks(lead, axis)
    follow = scatter_chunks(follow, axis)
    bit = 0
    while (1 << bit) < size:
        lead = scatter_step(lead, axis, bit)
        follow, _ = lax.optimization_barrier((follow, lead))
        follow = scatter_step(follow, axis, bit)
        bit += 1
    return lead[0], follow[0]


def shards(basis_values, aux_values, factors, frag_slot, dimer_pairs, counts, weights, metric_inv):
    highest = lax.Precision.HIGHEST
    basis_rows = basis_values[0]
    aux_block = aux_values[0]
    points = basis_rows.shape[0]
    naux = aux_block.shape[1]
    frag_basis = basis_rows.shape[1] // 2
    live_count = counts[0, 0]
    position = lax.iota(jnp.int32, points)
    live_weight = jnp.where(position < live_count, weights[0], jnp.zeros((), jnp.float32))
    gathered = xor_gather(factors, "dimer", 0)
    frag_ids = lax.iota(jnp.int32, frag_slot.shape[0])
    wanted = jnp.sum(
        jnp.where(frag_ids[None, :] == dimer_pairs[0][:, None], frag_slot[None, :], 0), axis=1
    )
    selector = (frag_ids[None, :] == wanted[:, None]).astype(jnp.bfloat16)
    chosen = jnp.einsum(
        "as,srk->ark", selector, gathered, preferred_element_type=jnp.float32
    ).astype(jnp.bfloat16)
    dimer_factors = xor_gather(chosen, "grid", 1)
    orb_first = jnp.dot(
        basis_rows[:, :frag_basis], dimer_factors[0], preferred_element_type=jnp.float32
    )
    orb_second = jnp.dot(
        basis_rows[:, frag_basis:], dimer_factors[1], preferred_element_type=jnp.float32
    )
    density = (
        jnp.sum(orb_first * orb_first, axis=1) + jnp.sum(orb_second * orb_second, axis=1)
    ) / (2.0 * dimer_factors.shape[2])
    exchange = -exchange_coeff * jnp.cbrt(density)
    weighted_density = live_weight * density
    high_rows, low_rows = split_rows(jnp.stack([weighted_density, live_weight]))
    projections = jnp.dot(
        jnp.concatenate([high_rows, low_rows]), aux_block, preferred_element_type=jnp.float32
    )
    fitted_part = projections[0] + projections[2]
    weight_part = projections[1] + projections[3]
    sums_part = jnp.stack([jnp.sum(live_weight * exchange), jnp.sum(live_weight)])
    payload = jnp.concatenate([fitted_part, weight_part, sums_part])
    totals = xor_sum(payload, "grid")
    fitted = totals[:naux]
    weight_projection = totals[naux : 2 * naux]
    exchange_total = totals[2 * naux]
    weight_sum = totals[2 * naux + 1]
    coef_rows = jnp.dot(metric_inv[0], fitted, precision=highest)
    coefficients = xor_gather(coef_rows, "grid", 0)
    coef_high, coef_low = split_rows(coefficients)
    coulomb_parts = jnp.dot(
        aux_block, jnp.stack([coef_high, coef_low], axis=1), preferred_element_type=jnp.float32
    )
    coulomb = coulomb_parts[:, 0] + coulomb_parts[:, 1]
    potential_total = jnp.dot(coefficients, weight_projection, precision=highest) + exchange_total
    average = potential_total / weight_sum
    potential = live_weight * (coulomb + exchange - average)
    weighted_basis = (basis_rows * potential[:, None]).astype(jnp.bfloat16)
    half_rows = frag_basis // lax.axis_size("grid")
    left_first = lax.slice_in_dim(weighted_basis, 0, half_rows * lax.axis_size("grid"), axis=1)
    left_second = lax.dynamic_slice_in_dim(
        weighted_basis, frag_basis, half_rows * lax.axis_size("grid"), 1
    )
    first_first = contract(left_first, basis_rows[:, :frag_basis])
    first_second = contract(left_first, basis_rows[:, frag_basis:])
    second_second = contract(left_second, basis_rows[:, frag_basis:])
    diagonal, own_cross = paired_scatter(
        jnp.stack([first_first, second_second], axis=1), first_second, "grid"
    )
    own_first = diagonal[:, 0]
    own_second = diagonal[:, 1]
    groups = lax.axis_size("dimer")
    me = lax.axis_index("dimer")
    zero = jnp.zeros((), jnp.float32)

    def piece(dest):
        return jnp.where(dimer_pairs[0, 0] == dest, own_first, zero) + jnp.where(
            dimer_pairs[0, 1] == dest, own_second, zero
        )

    frag_fock = piece(me)
    for shift in range(1, groups):
        sent = piece(lax.rem(me + shift, groups))
        frag_fock = frag_fock + lax.ppermute(
            sent, "dimer", [(i, (i + shift) % groups) for i in range(groups)]
        )
    return (frag_fock[None], own_cross[None])


def solution(mesh):
    placed = (
        P("dimer", "grid", None),
        P("dimer", "grid", None),
        P("dimer", "grid", None),
        P(),
        P("dimer", None),
        P("dimer", "grid"),
        P("dimer", "grid"),
        P("dimer", "grid", None),
    )
    return jax.shard_map(
        shards,
        mesh=mesh,
        in_specs=placed,
        out_specs=(P("dimer", "grid", None), P("dimer", "grid", None)),
        check_vma=False,
    )
```

```python
import jax
import jax.numpy as jnp
from jax import lax
from jax.sharding import PartitionSpec as P

exchange_coeff = 0.9847450218426964


def split_rows(rows):
    high_part = rows.astype(jnp.bfloat16)
    high_back = lax.optimization_barrier(high_part).astype(jnp.float32)
    low_part = (rows - high_back).astype(jnp.bfloat16)
    return high_part, low_part


def contract(left_side, right_side):
    numbers = (((0,), (0,)), ((), ()))
    return lax.dot_general(left_side, right_side, numbers, preferred_element_type=jnp.float32)


def xor_sum(value, axis):
    size = lax.axis_size(axis)
    if size & (size - 1):
        return lax.psum(value, axis)
    step = 1
    while step < size:
        value = value + lax.ppermute(value, axis, [(i, i ^ step) for i in range(size)])
        step *= 2
    return value


def xor_gather(value, axis, dim):
    size = lax.axis_size(axis)
    if size & (size - 1):
        plain = jnp.arange(size, dtype=jnp.int32)
        return lax.all_gather(value, axis, axis=dim, tiled=True), plain, plain
    me = lax.axis_index(axis)
    bits = size.bit_length() - 1
    for bit in reversed(range(bits)):
        other = lax.ppermute(value, axis, [(i, i ^ (1 << bit)) for i in range(size)])
        value = jnp.concatenate([value, other], axis=dim)
    flip = [sum(((p >> b) & 1) << (bits - 1 - b) for b in range(bits)) for p in range(size)]
    flipped_me = sum(((me >> b) & 1) << (bits - 1 - b) for b in range(bits))
    table = jnp.array(flip, jnp.int32)
    return value, jnp.bitwise_xor(table, me), jnp.bitwise_xor(table, flipped_me)


def in_order(value, holder, place, dim):
    size = holder.shape[0]
    shape = value.shape
    blocks = value.reshape(shape[:dim] + (size, shape[dim] // size) + shape[dim + 1 :])
    return jnp.take(blocks, place, axis=dim).reshape(shape)


def scatter_chunks(value, axis):
    size = lax.axis_size(axis)
    return value.reshape((size, value.shape[0] // size) + value.shape[1:])


def scatter_step(value, axis, bit):
    size = lax.axis_size(axis)
    mine = (lax.axis_index(axis) >> bit) & 1
    pairs = value.reshape((value.shape[0] // 2, 2) + value.shape[1:])
    keep = lax.dynamic_index_in_dim(pairs, mine, axis=1, keepdims=False)
    send = lax.dynamic_index_in_dim(pairs, 1 - mine, axis=1, keepdims=False)
    return keep + lax.ppermute(send, axis, [(i, i ^ (1 << bit)) for i in range(size)])


def paired_scatter(lead, follow, axis):
    size = lax.axis_size(axis)
    if size & (size - 1):
        return (
            lax.psum_scatter(lead, axis, scatter_dimension=0, tiled=True),
            lax.psum_scatter(follow, axis, scatter_dimension=0, tiled=True),
        )
    lead = scatter_chunks(lead, axis)
    follow = scatter_chunks(follow, axis)
    bit = 0
    while (1 << bit) < size:
        lead = scatter_step(lead, axis, bit)
        follow, _ = lax.optimization_barrier((follow, lead))
        follow = scatter_step(follow, axis, bit)
        bit += 1
    return lead[0], follow[0]


def shards(basis_values, aux_values, factors, frag_slot, dimer_pairs, counts, weights, metric_inv):
    highest = lax.Precision.HIGHEST
    basis_rows = basis_values[0]
    aux_block = aux_values[0]
    points = basis_rows.shape[0]
    naux = aux_block.shape[1]
    frag_basis = basis_rows.shape[1] // 2
    live_count = counts[0, 0]
    position = lax.iota(jnp.int32, points)
    live_weight = jnp.where(position < live_count, weights[0], jnp.zeros((), jnp.float32))
    gathered, slot_held, _ = xor_gather(factors, "dimer", 0)
    frag_ids = lax.iota(jnp.int32, frag_slot.shape[0])
    wanted = jnp.sum(
        jnp.where(frag_ids[None, :] == dimer_pairs[0][:, None], frag_slot[None, :], 0), axis=1
    )
    selector = (slot_held[None, :] == wanted[:, None]).astype(jnp.bfloat16)
    chosen = jnp.einsum(
        "as,srk->ark", selector, gathered, preferred_element_type=jnp.float32
    ).astype(jnp.bfloat16)
    dimer_factors = in_order(*xor_gather(chosen, "grid", 1), 1)
    orb_first = jnp.dot(
        basis_rows[:, :frag_basis], dimer_factors[0], preferred_element_type=jnp.float32
    )
    orb_second = jnp.dot(
        basis_rows[:, frag_basis:], dimer_factors[1], preferred_element_type=jnp.float32
    )
    density = (
        jnp.sum(orb_first * orb_first, axis=1) + jnp.sum(orb_second * orb_second, axis=1)
    ) / (2.0 * dimer_factors.shape[2])
    exchange = -exchange_coeff * jnp.cbrt(density)
    weighted_density = live_weight * density
    high_rows, low_rows = split_rows(jnp.stack([weighted_density, live_weight]))
    projections = jnp.dot(
        jnp.concatenate([high_rows, low_rows]), aux_block, preferred_element_type=jnp.float32
    )
    sums_part = jnp.stack([jnp.sum(live_weight * exchange), jnp.sum(live_weight)])
    first_lane = lax.broadcasted_iota(jnp.int32, (2, 128), 1) == 0
    payload = jnp.concatenate(
        [projections[:2] + projections[2:], jnp.where(first_lane, sums_part[:, None], 0.0)], axis=1
    )
    totals = xor_sum(payload, "grid")
    fitted = totals[0, :naux]
    weight_projection = totals[1, :naux]
    exchange_total = totals[0, naux]
    weight_sum = totals[1, naux]
    coef_rows = jnp.dot(metric_inv[0], fitted, precision=highest)
    coefficients = in_order(*xor_gather(coef_rows, "grid", 0), 0)
    coef_high, coef_low = split_rows(coefficients)
    coulomb_parts = jnp.dot(
        aux_block, jnp.stack([coef_high, coef_low], axis=1), preferred_element_type=jnp.float32
    )
    coulomb = coulomb_parts[:, 0] + coulomb_parts[:, 1]
    potential_total = jnp.dot(coefficients, weight_projection, precision=highest) + exchange_total
    average = potential_total / weight_sum
    potential = live_weight * (coulomb + exchange - average)
    weighted_basis = (basis_rows * potential[:, None]).astype(jnp.bfloat16)
    half_rows = frag_basis // lax.axis_size("grid")
    left_first = lax.slice_in_dim(weighted_basis, 0, half_rows * lax.axis_size("grid"), axis=1)
    left_second = lax.dynamic_slice_in_dim(
        weighted_basis, frag_basis, half_rows * lax.axis_size("grid"), 1
    )
    first_first = contract(left_first, basis_rows[:, :frag_basis])
    first_second = contract(left_first, basis_rows[:, frag_basis:])
    second_second = contract(left_second, basis_rows[:, frag_basis:])
    diagonal, own_cross = paired_scatter(
        jnp.stack([first_first, second_second], axis=1), first_second, "grid"
    )
    own_first = diagonal[:, 0]
    own_second = diagonal[:, 1]
    groups = lax.axis_size("dimer")
    me = lax.axis_index("dimer")
    zero = jnp.zeros((), jnp.float32)

    def piece(dest):
        return jnp.where(dimer_pairs[0, 0] == dest, own_first, zero) + jnp.where(
            dimer_pairs[0, 1] == dest, own_second, zero
        )

    frag_fock = piece(me)
    for shift in range(1, groups):
        sent = piece(lax.rem(me + shift, groups))
        frag_fock = frag_fock + lax.ppermute(
            sent, "dimer", [(i, (i + shift) % groups) for i in range(groups)]
        )
    return (frag_fock[None], own_cross[None])


def solution(mesh):
    placed = (
        P("dimer", "grid", None),
        P("dimer", "grid", None),
        P("dimer", "grid", None),
        P(),
        P("dimer", None),
        P("dimer", "grid"),
        P("dimer", "grid"),
        P("dimer", "grid", None),
    )
    return jax.shard_map(
        shards,
        mesh=mesh,
        in_specs=placed,
        out_specs=(P("dimer", "grid", None), P("dimer", "grid", None)),
        check_vma=False,
    )
```

```python
import jax
import jax.numpy as jnp
from jax import lax
from jax.sharding import PartitionSpec as P

exchange_coeff = 0.9847450218426964


def split_rows(rows):
    high_part = rows.astype(jnp.bfloat16)
    high_back = lax.optimization_barrier(high_part).astype(jnp.float32)
    low_part = (rows - high_back).astype(jnp.bfloat16)
    return high_part, low_part


def contract(left_side, right_side):
    numbers = (((0,), (0,)), ((), ()))
    return lax.dot_general(left_side, right_side, numbers, preferred_element_type=jnp.float32)


def xor_sum(value, axis):
    size = lax.axis_size(axis)
    if size & (size - 1):
        return lax.psum(value, axis)
    step = 1
    while step < size:
        value = value + lax.ppermute(value, axis, [(i, i ^ step) for i in range(size)])
        step *= 2
    return value


def xor_gather(value, axis, dim):
    size = lax.axis_size(axis)
    if size & (size - 1):
        plain = jnp.arange(size, dtype=jnp.int32)
        return lax.all_gather(value, axis, axis=dim, tiled=True), plain, plain
    me = lax.axis_index(axis)
    bits = size.bit_length() - 1
    for bit in reversed(range(bits)):
        other = lax.ppermute(value, axis, [(i, i ^ (1 << bit)) for i in range(size)])
        value = jnp.concatenate([value, other], axis=dim)
    flip = [sum(((p >> b) & 1) << (bits - 1 - b) for b in range(bits)) for p in range(size)]
    flipped_me = sum(((me >> b) & 1) << (bits - 1 - b) for b in range(bits))
    table = jnp.array(flip, jnp.int32)
    return value, jnp.bitwise_xor(table, me), jnp.bitwise_xor(table, flipped_me)


def in_order(value, holder, place, dim):
    size = holder.shape[0]
    shape = value.shape
    blocks = value.reshape(shape[:dim] + (size, shape[dim] // size) + shape[dim + 1 :])
    return jnp.take(blocks, place, axis=dim).reshape(shape)


def send_order(axis):
    size = lax.axis_size(axis)
    if size & (size - 1):
        return jnp.arange(size, dtype=jnp.int32)
    bits = size.bit_length() - 1
    flip = [sum(((p >> b) & 1) << (bits - 1 - b) for b in range(bits)) for p in range(size)]
    return jnp.bitwise_xor(jnp.array(flip, jnp.int32), lax.axis_index(axis))


def half_step(value, axis, bit):
    size = lax.axis_size(axis)
    half = value.shape[0] // 2
    sent = lax.ppermute(value[half:], axis, [(i, i ^ (1 << bit)) for i in range(size)])
    return value[:half] + sent


def paired_scatter(lead, follow, axis):
    size = lax.axis_size(axis)
    if size & (size - 1):
        return (
            lax.psum_scatter(lead, axis, scatter_dimension=0, tiled=True),
            lax.psum_scatter(follow, axis, scatter_dimension=0, tiled=True),
        )
    bit = 0
    while (1 << bit) < size:
        lead = half_step(lead, axis, bit)
        follow, _ = lax.optimization_barrier((follow, lead))
        follow = half_step(follow, axis, bit)
        bit += 1
    return lead, follow


def shards(basis_values, aux_values, factors, frag_slot, dimer_pairs, counts, weights, metric_inv):
    highest = lax.Precision.HIGHEST
    basis_rows = basis_values[0]
    aux_block = aux_values[0]
    points = basis_rows.shape[0]
    naux = aux_block.shape[1]
    frag_basis = basis_rows.shape[1] // 2
    live_count = counts[0, 0]
    position = lax.iota(jnp.int32, points)
    live_weight = jnp.where(position < live_count, weights[0], jnp.zeros((), jnp.float32))
    gathered, slot_held, _ = xor_gather(factors, "dimer", 0)
    frag_ids = lax.iota(jnp.int32, frag_slot.shape[0])
    wanted = jnp.sum(
        jnp.where(frag_ids[None, :] == dimer_pairs[0][:, None], frag_slot[None, :], 0), axis=1
    )
    selector = (slot_held[None, :] == wanted[:, None]).astype(jnp.bfloat16)
    chosen = jnp.einsum(
        "as,srk->ark", selector, gathered, preferred_element_type=jnp.float32
    ).astype(jnp.bfloat16)
    dimer_factors = in_order(*xor_gather(chosen, "grid", 1), 1)
    orb_first = jnp.dot(
        basis_rows[:, :frag_basis], dimer_factors[0], preferred_element_type=jnp.float32
    )
    orb_second = jnp.dot(
        basis_rows[:, frag_basis:], dimer_factors[1], preferred_element_type=jnp.float32
    )
    density = (
        jnp.sum(orb_first * orb_first, axis=1) + jnp.sum(orb_second * orb_second, axis=1)
    ) / (2.0 * dimer_factors.shape[2])
    exchange = -exchange_coeff * jnp.cbrt(density)
    weighted_density = live_weight * density
    high_rows, low_rows = split_rows(jnp.stack([weighted_density, live_weight]))
    projections = jnp.dot(
        jnp.concatenate([high_rows, low_rows]), aux_block, preferred_element_type=jnp.float32
    )
    sums_part = jnp.stack([jnp.sum(live_weight * exchange), jnp.sum(live_weight)])
    first_lane = lax.broadcasted_iota(jnp.int32, (2, 128), 1) == 0
    payload = jnp.concatenate(
        [projections[:2] + projections[2:], jnp.where(first_lane, sums_part[:, None], 0.0)], axis=1
    )
    totals = xor_sum(payload, "grid")
    fitted = totals[0, :naux]
    weight_projection = totals[1, :naux]
    exchange_total = totals[0, naux]
    weight_sum = totals[1, naux]
    coef_rows = jnp.dot(metric_inv[0], fitted, precision=highest)
    coefficients = in_order(*xor_gather(coef_rows, "grid", 0), 0)
    coef_high, coef_low = split_rows(coefficients)
    coulomb_parts = jnp.dot(
        aux_block, jnp.stack([coef_high, coef_low], axis=1), preferred_element_type=jnp.float32
    )
    coulomb = coulomb_parts[:, 0] + coulomb_parts[:, 1]
    potential_total = jnp.dot(coefficients, weight_projection, precision=highest) + exchange_total
    average = potential_total / weight_sum
    potential = live_weight * (coulomb + exchange - average)
    grid_size = lax.axis_size("grid")
    order = send_order("grid")
    blocked = basis_rows.reshape(points, 2, grid_size, frag_basis // grid_size)
    permuted_basis = jnp.take(blocked, order, axis=2).reshape(points, 2 * frag_basis)
    weighted_basis = (permuted_basis * potential[:, None]).astype(jnp.bfloat16)
    left_first = weighted_basis[:, :frag_basis]
    left_second = weighted_basis[:, frag_basis:]
    first_first = contract(left_first, basis_rows[:, :frag_basis])
    first_second = contract(left_first, basis_rows[:, frag_basis:])
    second_second = contract(left_second, basis_rows[:, frag_basis:])
    diagonal, own_cross = paired_scatter(
        jnp.stack([first_first, second_second], axis=1), first_second, "grid"
    )
    own_first = diagonal[:, 0]
    own_second = diagonal[:, 1]
    groups = lax.axis_size("dimer")
    me = lax.axis_index("dimer")
    zero = jnp.zeros((), jnp.float32)

    def piece(dest):
        return jnp.where(dimer_pairs[0, 0] == dest, own_first, zero) + jnp.where(
            dimer_pairs[0, 1] == dest, own_second, zero
        )

    frag_fock = piece(me)
    for shift in range(1, groups):
        sent = piece(lax.rem(me + shift, groups))
        frag_fock = frag_fock + lax.ppermute(
            sent, "dimer", [(i, (i + shift) % groups) for i in range(groups)]
        )
    return (frag_fock[None], own_cross[None])


def solution(mesh):
    placed = (
        P("dimer", "grid", None),
        P("dimer", "grid", None),
        P("dimer", "grid", None),
        P(),
        P("dimer", None),
        P("dimer", "grid"),
        P("dimer", "grid"),
        P("dimer", "grid", None),
    )
    return jax.shard_map(
        shards,
        mesh=mesh,
        in_specs=placed,
        out_specs=(P("dimer", "grid", None), P("dimer", "grid", None)),
        check_vma=False,
    )
```

```python
import jax
import jax.numpy as jnp
from jax import lax
from jax.sharding import PartitionSpec as P

exchange_coeff = 0.9847450218426964


def split_rows(rows):
    high_part = rows.astype(jnp.bfloat16)
    high_back = lax.optimization_barrier(high_part).astype(jnp.float32)
    low_part = (rows - high_back).astype(jnp.bfloat16)
    return high_part, low_part


def contract(left_side, right_side):
    numbers = (((0,), (0,)), ((), ()))
    return lax.dot_general(left_side, right_side, numbers, preferred_element_type=jnp.float32)


def xor_sum(value, axis):
    size = lax.axis_size(axis)
    if size & (size - 1):
        return lax.psum(value, axis)
    step = 1
    while step < size:
        value = value + lax.ppermute(value, axis, [(i, i ^ step) for i in range(size)])
        step *= 2
    return value


def xor_gather(value, axis, dim):
    size = lax.axis_size(axis)
    if size & (size - 1):
        plain = jnp.arange(size, dtype=jnp.int32)
        return lax.all_gather(value, axis, axis=dim, tiled=True), plain, plain
    me = lax.axis_index(axis)
    bits = size.bit_length() - 1
    for bit in reversed(range(bits)):
        other = lax.ppermute(value, axis, [(i, i ^ (1 << bit)) for i in range(size)])
        value = jnp.concatenate([value, other], axis=dim)
    flip = [sum(((p >> b) & 1) << (bits - 1 - b) for b in range(bits)) for p in range(size)]
    flipped_me = sum(((me >> b) & 1) << (bits - 1 - b) for b in range(bits))
    table = jnp.array(flip, jnp.int32)
    return value, jnp.bitwise_xor(table, me), jnp.bitwise_xor(table, flipped_me)


def in_order(value, holder, place, dim):
    size = holder.shape[0]
    shape = value.shape
    blocks = value.reshape(shape[:dim] + (size, shape[dim] // size) + shape[dim + 1 :])
    return jnp.take(blocks, place, axis=dim).reshape(shape)


def send_order(axis):
    size = lax.axis_size(axis)
    if size & (size - 1):
        return jnp.arange(size, dtype=jnp.int32)
    bits = size.bit_length() - 1
    flip = [sum(((p >> b) & 1) << (bits - 1 - b) for b in range(bits)) for p in range(size)]
    return jnp.bitwise_xor(jnp.array(flip, jnp.int32), lax.axis_index(axis))


def half_step(value, axis, bit):
    size = lax.axis_size(axis)
    half = value.shape[0] // 2
    sent = lax.ppermute(value[half:], axis, [(i, i ^ (1 << bit)) for i in range(size)])
    return value[:half] + sent


def paired_scatter(lead, follow, axis):
    size = lax.axis_size(axis)
    if size & (size - 1):
        return (
            lax.psum_scatter(lead, axis, scatter_dimension=0, tiled=True),
            lax.psum_scatter(follow, axis, scatter_dimension=0, tiled=True),
        )
    bit = 0
    while (1 << bit) < size:
        lead = half_step(lead, axis, bit)
        follow, _ = lax.optimization_barrier((follow, lead))
        follow = half_step(follow, axis, bit)
        bit += 1
    return lead, follow


def shards(basis_values, aux_values, factors, frag_slot, dimer_pairs, counts, weights, metric_inv):
    highest = lax.Precision.HIGHEST
    basis_rows = basis_values[0]
    aux_block = aux_values[0]
    points = basis_rows.shape[0]
    naux = aux_block.shape[1]
    frag_basis = basis_rows.shape[1] // 2
    live_count = counts[0, 0]
    position = lax.iota(jnp.int32, points)
    live_weight = jnp.where(position < live_count, weights[0], jnp.zeros((), jnp.float32))
    gathered, slot_held, _ = xor_gather(factors, "dimer", 0)
    frag_ids = lax.iota(jnp.int32, frag_slot.shape[0])
    wanted = jnp.sum(
        jnp.where(frag_ids[None, :] == dimer_pairs[0][:, None], frag_slot[None, :], 0), axis=1
    )
    selector = (slot_held[None, :] == wanted[:, None]).astype(jnp.bfloat16)
    chosen = jnp.einsum(
        "as,srk->ark", selector, gathered, preferred_element_type=jnp.float32
    ).astype(jnp.bfloat16)
    dimer_factors = in_order(*xor_gather(chosen, "grid", 1), 1)
    orb_first = jnp.dot(
        basis_rows[:, :frag_basis], dimer_factors[0], preferred_element_type=jnp.float32
    )
    orb_second = jnp.dot(
        basis_rows[:, frag_basis:], dimer_factors[1], preferred_element_type=jnp.float32
    )
    density = (
        jnp.sum(orb_first * orb_first, axis=1) + jnp.sum(orb_second * orb_second, axis=1)
    ) / (2.0 * dimer_factors.shape[2])
    exchange = -exchange_coeff * jnp.cbrt(density)
    weighted_density = live_weight * density
    high_rows, low_rows = split_rows(jnp.stack([weighted_density, live_weight]))
    projections = jnp.dot(
        jnp.concatenate([high_rows, low_rows]), aux_block, preferred_element_type=jnp.float32
    )
    sums_part = jnp.stack([jnp.sum(live_weight * exchange), jnp.sum(live_weight)])
    first_lane = lax.broadcasted_iota(jnp.int32, (2, 128), 1) == 0
    payload = jnp.concatenate(
        [projections[:2] + projections[2:], jnp.where(first_lane, sums_part[:, None], 0.0)], axis=1
    )
    totals = xor_sum(payload, "grid")
    fitted = totals[0, :naux]
    weight_projection = totals[1, :naux]
    exchange_total = totals[0, naux]
    weight_sum = totals[1, naux]
    coef_rows = jnp.dot(metric_inv[0], fitted, precision=highest)
    coefficients = in_order(*xor_gather(coef_rows, "grid", 0), 0)
    coef_high, coef_low = split_rows(coefficients)
    coulomb_parts = jnp.dot(
        aux_block, jnp.stack([coef_high, coef_low], axis=1), preferred_element_type=jnp.float32
    )
    coulomb = coulomb_parts[:, 0] + coulomb_parts[:, 1]
    potential_total = jnp.dot(coefficients, weight_projection, precision=highest) + exchange_total
    average = potential_total / weight_sum
    potential = live_weight * (coulomb + exchange - average)
    weighted_basis = (basis_rows * potential[:, None]).astype(jnp.bfloat16)
    left_first = weighted_basis[:, :frag_basis]
    left_second = weighted_basis[:, frag_basis:]
    first_first = contract(left_first, basis_rows[:, :frag_basis])
    first_second = contract(left_first, basis_rows[:, frag_basis:])
    second_second = contract(left_second, basis_rows[:, frag_basis:])
    grid_size = lax.axis_size("grid")
    order = send_order("grid")

    def in_send_order(rows):
        blocks = rows.reshape((grid_size, rows.shape[0] // grid_size) + rows.shape[1:])
        return jnp.take(blocks, order, axis=0).reshape(rows.shape)

    diagonal, own_cross = paired_scatter(
        in_send_order(jnp.stack([first_first, second_second], axis=1)),
        in_send_order(first_second),
        "grid",
    )
    own_first = diagonal[:, 0]
    own_second = diagonal[:, 1]
    groups = lax.axis_size("dimer")
    me = lax.axis_index("dimer")
    zero = jnp.zeros((), jnp.float32)

    def piece(dest):
        return jnp.where(dimer_pairs[0, 0] == dest, own_first, zero) + jnp.where(
            dimer_pairs[0, 1] == dest, own_second, zero
        )

    frag_fock = piece(me)
    for shift in range(1, groups):
        sent = piece(lax.rem(me + shift, groups))
        frag_fock = frag_fock + lax.ppermute(
            sent, "dimer", [(i, (i + shift) % groups) for i in range(groups)]
        )
    return (frag_fock[None], own_cross[None])


def solution(mesh):
    placed = (
        P("dimer", "grid", None),
        P("dimer", "grid", None),
        P("dimer", "grid", None),
        P(),
        P("dimer", None),
        P("dimer", "grid"),
        P("dimer", "grid"),
        P("dimer", "grid", None),
    )
    return jax.shard_map(
        shards,
        mesh=mesh,
        in_specs=placed,
        out_specs=(P("dimer", "grid", None), P("dimer", "grid", None)),
        check_vma=False,
    )
```

```python
import jax
import jax.numpy as jnp
from jax import lax
from jax.sharding import PartitionSpec as P

exchange_coeff = 0.9847450218426964


def split_rows(rows):
    high_part = rows.astype(jnp.bfloat16)
    high_back = lax.optimization_barrier(high_part).astype(jnp.float32)
    low_part = (rows - high_back).astype(jnp.bfloat16)
    return high_part, low_part


def contract(left_side, right_side):
    numbers = (((0,), (0,)), ((), ()))
    return lax.dot_general(left_side, right_side, numbers, preferred_element_type=jnp.float32)


def xor_sum(value, axis):
    size = lax.axis_size(axis)
    if size & (size - 1):
        return lax.psum(value, axis)
    step = 1
    while step < size:
        value = value + lax.ppermute(value, axis, [(i, i ^ step) for i in range(size)])
        step *= 2
    return value


def xor_gather(value, axis, dim):
    size = lax.axis_size(axis)
    if size & (size - 1):
        plain = jnp.arange(size, dtype=jnp.int32)
        return lax.all_gather(value, axis, axis=dim, tiled=True), plain, plain
    me = lax.axis_index(axis)
    bits = size.bit_length() - 1
    for bit in reversed(range(bits)):
        other = lax.ppermute(value, axis, [(i, i ^ (1 << bit)) for i in range(size)])
        value = jnp.concatenate([value, other], axis=dim)
    flip = [sum(((p >> b) & 1) << (bits - 1 - b) for b in range(bits)) for p in range(size)]
    flipped_me = sum(((me >> b) & 1) << (bits - 1 - b) for b in range(bits))
    table = jnp.array(flip, jnp.int32)
    return value, jnp.bitwise_xor(table, me), jnp.bitwise_xor(table, flipped_me)


def in_order(value, holder, place, dim):
    size = holder.shape[0]
    shape = value.shape
    blocks = value.reshape(shape[:dim] + (size, shape[dim] // size) + shape[dim + 1 :])
    return jnp.take(blocks, place, axis=dim).reshape(shape)


def scatter_chunks(value, axis):
    size = lax.axis_size(axis)
    return value.reshape((size, value.shape[0] // size) + value.shape[1:])


def scatter_step(value, axis, bit):
    size = lax.axis_size(axis)
    mine = (lax.axis_index(axis) >> bit) & 1
    pairs = value.reshape((value.shape[0] // 2, 2) + value.shape[1:])
    keep = lax.dynamic_index_in_dim(pairs, mine, axis=1, keepdims=False)
    send = lax.dynamic_index_in_dim(pairs, 1 - mine, axis=1, keepdims=False)
    return keep + lax.ppermute(send, axis, [(i, i ^ (1 << bit)) for i in range(size)])


def paired_scatter(lead, follow, axis):
    size = lax.axis_size(axis)
    if size & (size - 1):
        return (
            lax.psum_scatter(lead, axis, scatter_dimension=0, tiled=True),
            lax.psum_scatter(follow, axis, scatter_dimension=0, tiled=True),
        )
    lead = scatter_chunks(lead, axis)
    follow = scatter_chunks(follow, axis)
    bit = 0
    while (1 << bit) < size:
        lead = scatter_step(lead, axis, bit)
        follow, _ = lax.optimization_barrier((follow, lead))
        follow = scatter_step(follow, axis, bit)
        bit += 1
    return lead[0], follow[0]


def shards(basis_values, aux_values, factors, frag_slot, dimer_pairs, counts, weights, metric_inv):
    highest = lax.Precision.HIGHEST
    basis_rows = basis_values[0]
    aux_block = aux_values[0]
    points = basis_rows.shape[0]
    naux = aux_block.shape[1]
    frag_basis = basis_rows.shape[1] // 2
    live_count = counts[0, 0]
    position = lax.iota(jnp.int32, points)
    live_weight = jnp.where(position < live_count, weights[0], jnp.zeros((), jnp.float32))
    gathered, slot_held, _ = xor_gather(factors, "dimer", 0)
    frag_ids = lax.iota(jnp.int32, frag_slot.shape[0])
    wanted = jnp.sum(
        jnp.where(frag_ids[None, :] == dimer_pairs[0][:, None], frag_slot[None, :], 0), axis=1
    )
    selector = (slot_held[None, :] == wanted[:, None]).astype(jnp.bfloat16)
    chosen = jnp.einsum(
        "as,srk->ark", selector, gathered, preferred_element_type=jnp.float32
    ).astype(jnp.bfloat16)
    dimer_factors = in_order(*xor_gather(chosen, "grid", 1), 1)
    nocc = dimer_factors.shape[2]
    empty = jnp.zeros((frag_basis, nocc), jnp.bfloat16)
    block_factors = jnp.concatenate(
        [
            jnp.concatenate([dimer_factors[0], empty], axis=1),
            jnp.concatenate([empty, dimer_factors[1]], axis=1),
        ],
        axis=0,
    )
    orbitals = jnp.dot(basis_rows, block_factors, preferred_element_type=jnp.float32)
    density = jnp.sum(orbitals * orbitals, axis=1) / (2.0 * nocc)
    exchange = -exchange_coeff * jnp.cbrt(density)
    weighted_density = live_weight * density
    high_rows, low_rows = split_rows(jnp.stack([weighted_density, live_weight]))
    projections = jnp.dot(
        jnp.concatenate([high_rows, low_rows]), aux_block, preferred_element_type=jnp.float32
    )
    sums_part = jnp.stack([jnp.sum(live_weight * exchange), jnp.sum(live_weight)])
    first_lane = lax.broadcasted_iota(jnp.int32, (2, 128), 1) == 0
    payload = jnp.concatenate(
        [projections[:2] + projections[2:], jnp.where(first_lane, sums_part[:, None], 0.0)], axis=1
    )
    totals = xor_sum(payload, "grid")
    fitted = totals[0, :naux]
    weight_projection = totals[1, :naux]
    exchange_total = totals[0, naux]
    weight_sum = totals[1, naux]
    coef_rows = jnp.dot(metric_inv[0], fitted, precision=highest)
    coefficients = in_order(*xor_gather(coef_rows, "grid", 0), 0)
    coef_high, coef_low = split_rows(coefficients)
    coulomb_parts = jnp.dot(
        aux_block, jnp.stack([coef_high, coef_low], axis=1), preferred_element_type=jnp.float32
    )
    coulomb = coulomb_parts[:, 0] + coulomb_parts[:, 1]
    potential_total = jnp.dot(coefficients, weight_projection, precision=highest) + exchange_total
    average = potential_total / weight_sum
    potential = live_weight * (coulomb + exchange - average)
    weighted_basis = (basis_rows * potential[:, None]).astype(jnp.bfloat16)
    half_rows = frag_basis // lax.axis_size("grid")
    left_first = lax.slice_in_dim(weighted_basis, 0, half_rows * lax.axis_size("grid"), axis=1)
    left_second = lax.dynamic_slice_in_dim(
        weighted_basis, frag_basis, half_rows * lax.axis_size("grid"), 1
    )
    first_first = contract(left_first, basis_rows[:, :frag_basis])
    first_second = contract(left_first, basis_rows[:, frag_basis:])
    second_second = contract(left_second, basis_rows[:, frag_basis:])
    diagonal, own_cross = paired_scatter(
        jnp.stack([first_first, second_second], axis=1), first_second, "grid"
    )
    own_first = diagonal[:, 0]
    own_second = diagonal[:, 1]
    groups = lax.axis_size("dimer")
    me = lax.axis_index("dimer")
    zero = jnp.zeros((), jnp.float32)

    def piece(dest):
        return jnp.where(dimer_pairs[0, 0] == dest, own_first, zero) + jnp.where(
            dimer_pairs[0, 1] == dest, own_second, zero
        )

    frag_fock = piece(me)
    for shift in range(1, groups):
        sent = piece(lax.rem(me + shift, groups))
        frag_fock = frag_fock + lax.ppermute(
            sent, "dimer", [(i, (i + shift) % groups) for i in range(groups)]
        )
    return (frag_fock[None], own_cross[None])


def solution(mesh):
    placed = (
        P("dimer", "grid", None),
        P("dimer", "grid", None),
        P("dimer", "grid", None),
        P(),
        P("dimer", None),
        P("dimer", "grid"),
        P("dimer", "grid"),
        P("dimer", "grid", None),
    )
    return jax.shard_map(
        shards,
        mesh=mesh,
        in_specs=placed,
        out_specs=(P("dimer", "grid", None), P("dimer", "grid", None)),
        check_vma=False,
    )
```

```python
import jax
import jax.numpy as jnp
from jax import lax
from jax.sharding import PartitionSpec as P

exchange_coeff = 0.9847450218426964


def split_rows(rows):
    high_part = rows.astype(jnp.bfloat16)
    high_back = lax.optimization_barrier(high_part).astype(jnp.float32)
    low_part = (rows - high_back).astype(jnp.bfloat16)
    return high_part, low_part


def contract(left_side, right_side):
    numbers = (((0,), (0,)), ((), ()))
    return lax.dot_general(left_side, right_side, numbers, preferred_element_type=jnp.float32)


def xor_sum(value, axis):
    size = lax.axis_size(axis)
    if size & (size - 1):
        return lax.psum(value, axis)
    step = 1
    while step < size:
        value = value + lax.ppermute(value, axis, [(i, i ^ step) for i in range(size)])
        step *= 2
    return value


def xor_gather(value, axis, dim):
    size = lax.axis_size(axis)
    if size & (size - 1):
        plain = jnp.arange(size, dtype=jnp.int32)
        return lax.all_gather(value, axis, axis=dim, tiled=True), plain, plain
    me = lax.axis_index(axis)
    bits = size.bit_length() - 1
    for bit in reversed(range(bits)):
        other = lax.ppermute(value, axis, [(i, i ^ (1 << bit)) for i in range(size)])
        value = jnp.concatenate([value, other], axis=dim)
    flip = [sum(((p >> b) & 1) << (bits - 1 - b) for b in range(bits)) for p in range(size)]
    flipped_me = sum(((me >> b) & 1) << (bits - 1 - b) for b in range(bits))
    table = jnp.array(flip, jnp.int32)
    return value, jnp.bitwise_xor(table, me), jnp.bitwise_xor(table, flipped_me)


def in_order(value, holder, place, dim):
    size = holder.shape[0]
    shape = value.shape
    blocks = value.reshape(shape[:dim] + (size, shape[dim] // size) + shape[dim + 1 :])
    return jnp.take(blocks, place, axis=dim).reshape(shape)


def scatter_chunks(value, axis):
    size = lax.axis_size(axis)
    return value.reshape((size, value.shape[0] // size) + value.shape[1:])


def scatter_step(value, axis, bit):
    size = lax.axis_size(axis)
    mine = (lax.axis_index(axis) >> bit) & 1
    pairs = value.reshape((value.shape[0] // 2, 2) + value.shape[1:])
    keep = lax.dynamic_index_in_dim(pairs, mine, axis=1, keepdims=False)
    send = lax.dynamic_index_in_dim(pairs, 1 - mine, axis=1, keepdims=False)
    return keep + lax.ppermute(send, axis, [(i, i ^ (1 << bit)) for i in range(size)])


def chained_scatter(arrays, axis):
    size = lax.axis_size(axis)
    if size & (size - 1):
        return [lax.psum_scatter(a, axis, scatter_dimension=0, tiled=True) for a in arrays]
    arrays = [scatter_chunks(a, axis) for a in arrays]
    bit = 0
    while (1 << bit) < size:
        for index in range(len(arrays)):
            if index:
                arrays[index], _ = lax.optimization_barrier((arrays[index], arrays[index - 1]))
            arrays[index] = scatter_step(arrays[index], axis, bit)
        bit += 1
    return [a[0] for a in arrays]


def shards(basis_values, aux_values, factors, frag_slot, dimer_pairs, counts, weights, metric_inv):
    highest = lax.Precision.HIGHEST
    basis_rows = basis_values[0]
    aux_block = aux_values[0]
    points = basis_rows.shape[0]
    naux = aux_block.shape[1]
    frag_basis = basis_rows.shape[1] // 2
    live_count = counts[0, 0]
    position = lax.iota(jnp.int32, points)
    live_weight = jnp.where(position < live_count, weights[0], jnp.zeros((), jnp.float32))
    gathered, slot_held, _ = xor_gather(factors, "dimer", 0)
    frag_ids = lax.iota(jnp.int32, frag_slot.shape[0])
    wanted = jnp.sum(
        jnp.where(frag_ids[None, :] == dimer_pairs[0][:, None], frag_slot[None, :], 0), axis=1
    )
    selector = (slot_held[None, :] == wanted[:, None]).astype(jnp.bfloat16)
    chosen = jnp.einsum(
        "as,srk->ark", selector, gathered, preferred_element_type=jnp.float32
    ).astype(jnp.bfloat16)
    dimer_factors = in_order(*xor_gather(chosen, "grid", 1), 1)
    nocc = dimer_factors.shape[2]
    empty = jnp.zeros((frag_basis, nocc), jnp.bfloat16)
    block_factors = jnp.concatenate(
        [
            jnp.concatenate([dimer_factors[0], empty], axis=1),
            jnp.concatenate([empty, dimer_factors[1]], axis=1),
        ],
        axis=0,
    )
    orbitals = jnp.dot(basis_rows, block_factors, preferred_element_type=jnp.float32)
    density = jnp.sum(orbitals * orbitals, axis=1) / (2.0 * nocc)
    exchange = -exchange_coeff * jnp.cbrt(density)
    weighted_density = live_weight * density
    high_rows, low_rows = split_rows(jnp.stack([weighted_density, live_weight]))
    projections = jnp.dot(
        jnp.concatenate([high_rows, low_rows]), aux_block, preferred_element_type=jnp.float32
    )
    sums_part = jnp.stack([jnp.sum(live_weight * exchange), jnp.sum(live_weight)])
    first_lane = lax.broadcasted_iota(jnp.int32, (2, 128), 1) == 0
    payload = jnp.concatenate(
        [projections[:2] + projections[2:], jnp.where(first_lane, sums_part[:, None], 0.0)], axis=1
    )
    totals = xor_sum(payload, "grid")
    fitted = totals[0, :naux]
    weight_projection = totals[1, :naux]
    exchange_total = totals[0, naux]
    weight_sum = totals[1, naux]
    coef_rows = jnp.dot(metric_inv[0], fitted, precision=highest)
    coefficients = in_order(*xor_gather(coef_rows, "grid", 0), 0)
    coef_high, coef_low = split_rows(coefficients)
    coulomb_parts = jnp.dot(
        aux_block, jnp.stack([coef_high, coef_low], axis=1), preferred_element_type=jnp.float32
    )
    coulomb = coulomb_parts[:, 0] + coulomb_parts[:, 1]
    potential_total = jnp.dot(coefficients, weight_projection, precision=highest) + exchange_total
    average = potential_total / weight_sum
    potential = live_weight * (coulomb + exchange - average)
    weighted_basis = (basis_rows * potential[:, None]).astype(jnp.bfloat16)
    half_rows = frag_basis // lax.axis_size("grid")
    left_first = lax.slice_in_dim(weighted_basis, 0, half_rows * lax.axis_size("grid"), axis=1)
    left_second = lax.dynamic_slice_in_dim(
        weighted_basis, frag_basis, half_rows * lax.axis_size("grid"), 1
    )
    first_first = contract(left_first, basis_rows[:, :frag_basis])
    first_second = contract(left_first, basis_rows[:, frag_basis:])
    second_second = contract(left_second, basis_rows[:, frag_basis:])
    own_first, own_second, own_cross = chained_scatter(
        [first_first, second_second, first_second], "grid"
    )
    groups = lax.axis_size("dimer")
    me = lax.axis_index("dimer")
    zero = jnp.zeros((), jnp.float32)

    def piece(dest):
        return jnp.where(dimer_pairs[0, 0] == dest, own_first, zero) + jnp.where(
            dimer_pairs[0, 1] == dest, own_second, zero
        )

    frag_fock = piece(me)
    for shift in range(1, groups):
        sent = piece(lax.rem(me + shift, groups))
        frag_fock = frag_fock + lax.ppermute(
            sent, "dimer", [(i, (i + shift) % groups) for i in range(groups)]
        )
    return (frag_fock[None], own_cross[None])


def solution(mesh):
    placed = (
        P("dimer", "grid", None),
        P("dimer", "grid", None),
        P("dimer", "grid", None),
        P(),
        P("dimer", None),
        P("dimer", "grid"),
        P("dimer", "grid"),
        P("dimer", "grid", None),
    )
    return jax.shard_map(
        shards,
        mesh=mesh,
        in_specs=placed,
        out_specs=(P("dimer", "grid", None), P("dimer", "grid", None)),
        check_vma=False,
    )
```

```python
import jax
import jax.numpy as jnp
from jax import lax
from jax.experimental import pallas as pl
from jax.sharding import PartitionSpec as P

exchange_coeff = 0.9847450218426964


def split_rows(rows):
    high_part = rows.astype(jnp.bfloat16)
    high_back = lax.optimization_barrier(high_part).astype(jnp.float32)
    low_part = (rows - high_back).astype(jnp.bfloat16)
    return high_part, low_part


def contract(left_side, right_side):
    numbers = (((0,), (0,)), ((), ()))
    return lax.dot_general(left_side, right_side, numbers, preferred_element_type=jnp.float32)


def xor_sum(value, axis):
    size = lax.axis_size(axis)
    if size & (size - 1):
        return lax.psum(value, axis)
    step = 1
    while step < size:
        value = value + lax.ppermute(value, axis, [(i, i ^ step) for i in range(size)])
        step *= 2
    return value


def xor_gather(value, axis, dim):
    size = lax.axis_size(axis)
    if size & (size - 1):
        plain = jnp.arange(size, dtype=jnp.int32)
        return lax.all_gather(value, axis, axis=dim, tiled=True), plain, plain
    me = lax.axis_index(axis)
    bits = size.bit_length() - 1
    for bit in reversed(range(bits)):
        other = lax.ppermute(value, axis, [(i, i ^ (1 << bit)) for i in range(size)])
        value = jnp.concatenate([value, other], axis=dim)
    flip = [sum(((p >> b) & 1) << (bits - 1 - b) for b in range(bits)) for p in range(size)]
    flipped_me = sum(((me >> b) & 1) << (bits - 1 - b) for b in range(bits))
    table = jnp.array(flip, jnp.int32)
    return value, jnp.bitwise_xor(table, me), jnp.bitwise_xor(table, flipped_me)


def in_order(value, holder, place, dim):
    size = holder.shape[0]
    shape = value.shape
    blocks = value.reshape(shape[:dim] + (size, shape[dim] // size) + shape[dim + 1 :])
    return jnp.take(blocks, place, axis=dim).reshape(shape)


def scatter_chunks(value, axis):
    size = lax.axis_size(axis)
    return value.reshape((size, value.shape[0] // size) + value.shape[1:])


def scatter_step(value, axis, bit):
    size = lax.axis_size(axis)
    mine = (lax.axis_index(axis) >> bit) & 1
    pairs = value.reshape((value.shape[0] // 2, 2) + value.shape[1:])
    keep = lax.dynamic_index_in_dim(pairs, mine, axis=1, keepdims=False)
    send = lax.dynamic_index_in_dim(pairs, 1 - mine, axis=1, keepdims=False)
    return keep + lax.ppermute(send, axis, [(i, i ^ (1 << bit)) for i in range(size)])


def paired_scatter(lead, follow, axis):
    size = lax.axis_size(axis)
    if size & (size - 1):
        return (
            lax.psum_scatter(lead, axis, scatter_dimension=0, tiled=True),
            lax.psum_scatter(follow, axis, scatter_dimension=0, tiled=True),
        )
    lead = scatter_chunks(lead, axis)
    follow = scatter_chunks(follow, axis)
    bit = 0
    while (1 << bit) < size:
        lead = scatter_step(lead, axis, bit)
        follow, _ = lax.optimization_barrier((follow, lead))
        follow = scatter_step(follow, axis, bit)
        bit += 1
    return lead[0], follow[0]


def coulomb_kernel(aux_ref, coef_ref, out_ref):
    out_ref[...] = jnp.dot(aux_ref[...], coef_ref[...], preferred_element_type=jnp.float32)


def coulomb_columns(aux_block, coef_columns):
    points, naux = aux_block.shape
    width = coef_columns.shape[1]
    tile = 256 if points % 256 == 0 else points
    return pl.pallas_call(
        coulomb_kernel,
        grid=(points // tile,),
        in_specs=[
            pl.BlockSpec((tile, naux), lambda i: (i, 0)),
            pl.BlockSpec((naux, width), lambda i: (0, 0)),
        ],
        out_specs=pl.BlockSpec((tile, width), lambda i: (i, 0)),
        out_shape=jax.ShapeDtypeStruct((points, width), jnp.float32),
        cost_estimate=pl.CostEstimate(
            flops=2 * points * naux * width,
            bytes_accessed=points * naux * 2 + naux * width * 2 + points * width * 4,
            transcendentals=0,
        ),
    )(aux_block, coef_columns)


def shards(basis_values, aux_values, factors, frag_slot, dimer_pairs, counts, weights, metric_inv):
    highest = lax.Precision.HIGHEST
    basis_rows = basis_values[0]
    aux_block = aux_values[0]
    points = basis_rows.shape[0]
    naux = aux_block.shape[1]
    frag_basis = basis_rows.shape[1] // 2
    live_count = counts[0, 0]
    position = lax.iota(jnp.int32, points)
    live_weight = jnp.where(position < live_count, weights[0], jnp.zeros((), jnp.float32))
    gathered, slot_held, _ = xor_gather(factors, "dimer", 0)
    frag_ids = lax.iota(jnp.int32, frag_slot.shape[0])
    wanted = jnp.sum(
        jnp.where(frag_ids[None, :] == dimer_pairs[0][:, None], frag_slot[None, :], 0), axis=1
    )
    selector = (slot_held[None, :] == wanted[:, None]).astype(jnp.bfloat16)
    chosen = jnp.einsum(
        "as,srk->ark", selector, gathered, preferred_element_type=jnp.float32
    ).astype(jnp.bfloat16)
    dimer_factors = in_order(*xor_gather(chosen, "grid", 1), 1)
    nocc = dimer_factors.shape[2]
    empty = jnp.zeros((frag_basis, nocc), jnp.bfloat16)
    block_factors = jnp.concatenate(
        [
            jnp.concatenate([dimer_factors[0], empty], axis=1),
            jnp.concatenate([empty, dimer_factors[1]], axis=1),
        ],
        axis=0,
    )
    orbitals = jnp.dot(basis_rows, block_factors, preferred_element_type=jnp.float32)
    density = jnp.sum(orbitals * orbitals, axis=1) / (2.0 * nocc)
    exchange = -exchange_coeff * jnp.cbrt(density)
    weighted_density = live_weight * density
    high_rows, low_rows = split_rows(jnp.stack([weighted_density, live_weight]))
    projections = jnp.dot(
        jnp.concatenate([high_rows, low_rows]), aux_block, preferred_element_type=jnp.float32
    )
    sums_part = jnp.stack([jnp.sum(live_weight * exchange), jnp.sum(live_weight)])
    first_lane = lax.broadcasted_iota(jnp.int32, (2, 128), 1) == 0
    payload = jnp.concatenate(
        [projections[:2] + projections[2:], jnp.where(first_lane, sums_part[:, None], 0.0)], axis=1
    )
    totals = xor_sum(payload, "grid")
    fitted = totals[0, :naux]
    weight_projection = totals[1, :naux]
    exchange_total = totals[0, naux]
    weight_sum = totals[1, naux]
    coef_rows = jnp.dot(metric_inv[0], fitted, precision=highest)
    coefficients = in_order(*xor_gather(coef_rows, "grid", 0), 0)
    coef_high, coef_low = split_rows(coefficients)
    first_two = lax.broadcasted_iota(jnp.int32, (naux, 128), 1)
    coef_columns = jnp.where(
        first_two == 0,
        coef_high[:, None],
        jnp.where(first_two == 1, coef_low[:, None], jnp.zeros((), jnp.bfloat16)),
    )
    coulomb_parts = coulomb_columns(aux_block, coef_columns)
    coulomb = coulomb_parts[:, 0] + coulomb_parts[:, 1]
    potential_total = jnp.dot(coefficients, weight_projection, precision=highest) + exchange_total
    average = potential_total / weight_sum
    potential = live_weight * (coulomb + exchange - average)
    weighted_basis = (basis_rows * potential[:, None]).astype(jnp.bfloat16)
    half_rows = frag_basis // lax.axis_size("grid")
    left_first = lax.slice_in_dim(weighted_basis, 0, half_rows * lax.axis_size("grid"), axis=1)
    left_second = lax.dynamic_slice_in_dim(
        weighted_basis, frag_basis, half_rows * lax.axis_size("grid"), 1
    )
    first_first = contract(left_first, basis_rows[:, :frag_basis])
    first_second = contract(left_first, basis_rows[:, frag_basis:])
    second_second = contract(left_second, basis_rows[:, frag_basis:])
    diagonal, own_cross = paired_scatter(
        jnp.stack([first_first, second_second], axis=1), first_second, "grid"
    )
    own_first = diagonal[:, 0]
    own_second = diagonal[:, 1]
    groups = lax.axis_size("dimer")
    me = lax.axis_index("dimer")
    zero = jnp.zeros((), jnp.float32)

    def piece(dest):
        return jnp.where(dimer_pairs[0, 0] == dest, own_first, zero) + jnp.where(
            dimer_pairs[0, 1] == dest, own_second, zero
        )

    frag_fock = piece(me)
    for shift in range(1, groups):
        sent = piece(lax.rem(me + shift, groups))
        frag_fock = frag_fock + lax.ppermute(
            sent, "dimer", [(i, (i + shift) % groups) for i in range(groups)]
        )
    return (frag_fock[None], own_cross[None])


def solution(mesh):
    placed = (
        P("dimer", "grid", None),
        P("dimer", "grid", None),
        P("dimer", "grid", None),
        P(),
        P("dimer", None),
        P("dimer", "grid"),
        P("dimer", "grid"),
        P("dimer", "grid", None),
    )
    return jax.shard_map(
        shards,
        mesh=mesh,
        in_specs=placed,
        out_specs=(P("dimer", "grid", None), P("dimer", "grid", None)),
        check_vma=False,
    )
```

```python
import jax
import jax.numpy as jnp
from jax import lax
from jax.sharding import PartitionSpec as P

exchange_coeff = 0.9847450218426964


def split_rows(rows):
    high_part = rows.astype(jnp.bfloat16)
    high_back = lax.optimization_barrier(high_part).astype(jnp.float32)
    low_part = (rows - high_back).astype(jnp.bfloat16)
    return high_part, low_part


def contract(left_side, right_side):
    numbers = (((0,), (0,)), ((), ()))
    return lax.dot_general(left_side, right_side, numbers, preferred_element_type=jnp.float32)


def xor_sum(value, axis):
    size = lax.axis_size(axis)
    if size & (size - 1):
        return lax.psum(value, axis)
    step = 1
    while step < size:
        value = value + lax.ppermute(value, axis, [(i, i ^ step) for i in range(size)])
        step *= 2
    return value


def xor_gather(value, axis, dim):
    size = lax.axis_size(axis)
    if size & (size - 1):
        plain = jnp.arange(size, dtype=jnp.int32)
        return lax.all_gather(value, axis, axis=dim, tiled=True), plain, plain
    me = lax.axis_index(axis)
    bits = size.bit_length() - 1
    for bit in reversed(range(bits)):
        other = lax.ppermute(value, axis, [(i, i ^ (1 << bit)) for i in range(size)])
        value = jnp.concatenate([value, other], axis=dim)
    flip = [sum(((p >> b) & 1) << (bits - 1 - b) for b in range(bits)) for p in range(size)]
    flipped_me = sum(((me >> b) & 1) << (bits - 1 - b) for b in range(bits))
    table = jnp.array(flip, jnp.int32)
    return value, jnp.bitwise_xor(table, me), jnp.bitwise_xor(table, flipped_me)


def in_order(value, holder, place, dim):
    size = holder.shape[0]
    shape = value.shape
    blocks = value.reshape(shape[:dim] + (size, shape[dim] // size) + shape[dim + 1 :])
    return jnp.take(blocks, place, axis=dim).reshape(shape)


def scatter_chunks(value, axis):
    size = lax.axis_size(axis)
    return value.reshape((size, value.shape[0] // size) + value.shape[1:])


def scatter_step(value, axis, bit):
    size = lax.axis_size(axis)
    mine = (lax.axis_index(axis) >> bit) & 1
    pairs = value.reshape((value.shape[0] // 2, 2) + value.shape[1:])
    keep = lax.dynamic_index_in_dim(pairs, mine, axis=1, keepdims=False)
    send = lax.dynamic_index_in_dim(pairs, 1 - mine, axis=1, keepdims=False)
    return keep + lax.ppermute(send, axis, [(i, i ^ (1 << bit)) for i in range(size)])


def paired_scatter(lead, follow, axis):
    size = lax.axis_size(axis)
    if size & (size - 1):
        return (
            lax.psum_scatter(lead, axis, scatter_dimension=0, tiled=True),
            lax.psum_scatter(follow, axis, scatter_dimension=0, tiled=True),
        )
    lead = scatter_chunks(lead, axis)
    follow = scatter_chunks(follow, axis)
    bit = 0
    while (1 << bit) < size:
        lead = scatter_step(lead, axis, bit)
        follow, _ = lax.optimization_barrier((follow, lead))
        follow = scatter_step(follow, axis, bit)
        bit += 1
    return lead[0], follow[0]


def shards(basis_values, aux_values, factors, frag_slot, dimer_pairs, counts, weights, metric_inv):
    highest = lax.Precision.HIGHEST
    basis_rows = basis_values[0]
    aux_block = aux_values[0]
    points = basis_rows.shape[0]
    naux = aux_block.shape[1]
    frag_basis = basis_rows.shape[1] // 2
    live_count = counts[0, 0]
    position = lax.iota(jnp.int32, points)
    live_weight = jnp.where(position < live_count, weights[0], jnp.zeros((), jnp.float32))
    gathered, slot_held, _ = xor_gather(factors[0], "dimer", 0)
    gathered = gathered.reshape((slot_held.shape[0],) + factors.shape[1:])
    frag_ids = lax.iota(jnp.int32, frag_slot.shape[0])
    wanted = jnp.sum(
        jnp.where(frag_ids[None, :] == dimer_pairs[0][:, None], frag_slot[None, :], 0), axis=1
    )
    selector = (slot_held[None, :] == wanted[:, None]).astype(jnp.bfloat16)
    chosen = jnp.einsum(
        "as,srk->ark", selector, gathered, preferred_element_type=jnp.float32
    ).astype(jnp.bfloat16)
    dimer_factors = in_order(*xor_gather(chosen, "grid", 1), 1)
    nocc = dimer_factors.shape[2]
    empty = jnp.zeros((frag_basis, nocc), jnp.bfloat16)
    block_factors = jnp.concatenate(
        [
            jnp.concatenate([dimer_factors[0], empty], axis=1),
            jnp.concatenate([empty, dimer_factors[1]], axis=1),
        ],
        axis=0,
    )
    orbitals = jnp.dot(basis_rows, block_factors, preferred_element_type=jnp.float32)
    density = jnp.sum(orbitals * orbitals, axis=1) / (2.0 * nocc)
    exchange = -exchange_coeff * jnp.cbrt(density)
    weighted_density = live_weight * density
    high_rows, low_rows = split_rows(jnp.stack([weighted_density, live_weight]))
    projections = jnp.dot(
        jnp.concatenate([high_rows, low_rows]), aux_block, preferred_element_type=jnp.float32
    )
    sums_part = jnp.stack([jnp.sum(live_weight * exchange), jnp.sum(live_weight)])
    first_lane = lax.broadcasted_iota(jnp.int32, (2, 128), 1) == 0
    payload = jnp.concatenate(
        [projections[:2] + projections[2:], jnp.where(first_lane, sums_part[:, None], 0.0)], axis=1
    )
    totals = xor_sum(payload, "grid")
    fitted = totals[0, :naux]
    weight_projection = totals[1, :naux]
    exchange_total = totals[0, naux]
    weight_sum = totals[1, naux]
    coef_rows = jnp.dot(metric_inv[0], fitted, precision=highest)
    coefficients = in_order(*xor_gather(coef_rows, "grid", 0), 0)
    coef_high, coef_low = split_rows(coefficients)
    coulomb_parts = jnp.dot(
        aux_block, jnp.stack([coef_high, coef_low], axis=1), preferred_element_type=jnp.float32
    )
    coulomb = coulomb_parts[:, 0] + coulomb_parts[:, 1]
    potential_total = jnp.dot(coefficients, weight_projection, precision=highest) + exchange_total
    average = potential_total / weight_sum
    potential = live_weight * (coulomb + exchange - average)
    weighted_basis = (basis_rows * potential[:, None]).astype(jnp.bfloat16)
    half_rows = frag_basis // lax.axis_size("grid")
    left_first = lax.slice_in_dim(weighted_basis, 0, half_rows * lax.axis_size("grid"), axis=1)
    left_second = lax.dynamic_slice_in_dim(
        weighted_basis, frag_basis, half_rows * lax.axis_size("grid"), 1
    )
    first_first = contract(left_first, basis_rows[:, :frag_basis])
    first_second = contract(left_first, basis_rows[:, frag_basis:])
    second_second = contract(left_second, basis_rows[:, frag_basis:])
    diagonal, own_cross = paired_scatter(
        jnp.stack([first_first, second_second], axis=1), first_second, "grid"
    )
    own_first = diagonal[:, 0]
    own_second = diagonal[:, 1]
    groups = lax.axis_size("dimer")
    me = lax.axis_index("dimer")
    zero = jnp.zeros((), jnp.float32)

    def piece(dest):
        return jnp.where(dimer_pairs[0, 0] == dest, own_first, zero) + jnp.where(
            dimer_pairs[0, 1] == dest, own_second, zero
        )

    frag_fock = piece(me)
    for shift in range(1, groups):
        sent = piece(lax.rem(me + shift, groups))
        frag_fock = frag_fock + lax.ppermute(
            sent, "dimer", [(i, (i + shift) % groups) for i in range(groups)]
        )
    return (frag_fock[None], own_cross[None])


def solution(mesh):
    placed = (
        P("dimer", "grid", None),
        P("dimer", "grid", None),
        P("dimer", "grid", None),
        P(),
        P("dimer", None),
        P("dimer", "grid"),
        P("dimer", "grid"),
        P("dimer", "grid", None),
    )
    return jax.shard_map(
        shards,
        mesh=mesh,
        in_specs=placed,
        out_specs=(P("dimer", "grid", None), P("dimer", "grid", None)),
        check_vma=False,
    )
```

```python
import jax
import jax.numpy as jnp
from jax import lax
from jax.sharding import PartitionSpec as P

exchange_coeff = 0.9847450218426964


def split_rows(rows):
    high_part = rows.astype(jnp.bfloat16)
    high_back = lax.optimization_barrier(high_part).astype(jnp.float32)
    low_part = (rows - high_back).astype(jnp.bfloat16)
    return high_part, low_part


def contract(left_side, right_side):
    numbers = (((0,), (0,)), ((), ()))
    return lax.dot_general(left_side, right_side, numbers, preferred_element_type=jnp.float32)


def xor_sum(value, axis):
    size = lax.axis_size(axis)
    if size & (size - 1):
        return lax.psum(value, axis)
    step = 1
    while step < size:
        value = value + lax.ppermute(value, axis, [(i, i ^ step) for i in range(size)])
        step *= 2
    return value


def xor_gather(value, axis, dim):
    size = lax.axis_size(axis)
    if size & (size - 1):
        plain = jnp.arange(size, dtype=jnp.int32)
        return lax.all_gather(value, axis, axis=dim, tiled=True), plain, plain
    me = lax.axis_index(axis)
    bits = size.bit_length() - 1
    for bit in reversed(range(bits)):
        other = lax.ppermute(value, axis, [(i, i ^ (1 << bit)) for i in range(size)])
        value = jnp.concatenate([value, other], axis=dim)
    flip = [sum(((p >> b) & 1) << (bits - 1 - b) for b in range(bits)) for p in range(size)]
    flipped_me = sum(((me >> b) & 1) << (bits - 1 - b) for b in range(bits))
    table = jnp.array(flip, jnp.int32)
    return value, jnp.bitwise_xor(table, me), jnp.bitwise_xor(table, flipped_me)


def in_order(value, holder, place, dim):
    size = holder.shape[0]
    shape = value.shape
    blocks = value.reshape(shape[:dim] + (size, shape[dim] // size) + shape[dim + 1 :])
    return jnp.take(blocks, place, axis=dim).reshape(shape)


def scatter_chunks(value, axis):
    size = lax.axis_size(axis)
    return value.reshape((size, value.shape[0] // size) + value.shape[1:])


def scatter_step(value, axis, bit):
    size = lax.axis_size(axis)
    mine = (lax.axis_index(axis) >> bit) & 1
    pairs = value.reshape((value.shape[0] // 2, 2) + value.shape[1:])
    keep = lax.dynamic_index_in_dim(pairs, mine, axis=1, keepdims=False)
    send = lax.dynamic_index_in_dim(pairs, 1 - mine, axis=1, keepdims=False)
    return keep + lax.ppermute(send, axis, [(i, i ^ (1 << bit)) for i in range(size)])


def paired_scatter(lead, follow, axis):
    size = lax.axis_size(axis)
    if size & (size - 1):
        return (
            lax.psum_scatter(lead, axis, scatter_dimension=0, tiled=True),
            lax.psum_scatter(follow, axis, scatter_dimension=0, tiled=True),
        )
    lead = scatter_chunks(lead, axis)
    follow = scatter_chunks(follow, axis)
    bit = 0
    while (1 << bit) < size:
        lead = scatter_step(lead, axis, bit)
        follow, _ = lax.optimization_barrier((follow, lead))
        follow = scatter_step(follow, axis, bit)
        bit += 1
    return lead[0], follow[0]


def shards(basis_values, aux_values, factors, frag_slot, dimer_pairs, counts, weights, metric_inv):
    highest = lax.Precision.HIGHEST
    basis_rows = basis_values[0]
    aux_block = aux_values[0]
    points = basis_rows.shape[0]
    naux = aux_block.shape[1]
    frag_basis = basis_rows.shape[1] // 2
    live_count = counts[0, 0]
    position = lax.iota(jnp.int32, points)
    live_weight = jnp.where(position < live_count, weights[0], jnp.zeros((), jnp.float32))
    gathered, slot_held, _ = xor_gather(factors, "dimer", 0)
    frag_ids = lax.iota(jnp.int32, frag_slot.shape[0])
    wanted = jnp.sum(
        jnp.where(frag_ids[None, :] == dimer_pairs[0][:, None], frag_slot[None, :], 0), axis=1
    )
    selector = (slot_held[None, :] == wanted[:, None]).astype(jnp.bfloat16)
    chosen = jnp.einsum(
        "as,srk->ark", selector, gathered, preferred_element_type=jnp.float32
    ).astype(jnp.bfloat16)
    dimer_factors = in_order(*xor_gather(chosen, "grid", 1), 1)
    nocc = dimer_factors.shape[2]
    empty = jnp.zeros((frag_basis, nocc), jnp.bfloat16)
    block_factors = jnp.concatenate(
        [
            jnp.concatenate([dimer_factors[0], empty], axis=1),
            jnp.concatenate([empty, dimer_factors[1]], axis=1),
        ],
        axis=0,
    )
    orbitals = jnp.dot(basis_rows, block_factors, preferred_element_type=jnp.float32)
    density = jnp.sum(orbitals * orbitals, axis=1) / (2.0 * nocc)
    exchange = -exchange_coeff * jnp.cbrt(density)
    weighted_density = live_weight * density
    high_rows, low_rows = split_rows(jnp.stack([weighted_density, live_weight]))
    projections = jnp.dot(
        jnp.concatenate([high_rows, low_rows]), aux_block, preferred_element_type=jnp.float32
    )
    sums_part = jnp.stack([jnp.sum(live_weight * exchange), jnp.sum(live_weight)])
    first_lane = lax.broadcasted_iota(jnp.int32, (2, 128), 1) == 0
    payload = jnp.concatenate(
        [projections[:2] + projections[2:], jnp.where(first_lane, sums_part[:, None], 0.0)], axis=1
    )
    totals = xor_sum(payload, "grid")
    fitted = totals[0, :naux]
    weight_projection = totals[1, :naux]
    exchange_total = totals[0, naux : naux + 1]
    weight_sum = totals[1, naux : naux + 1]
    coef_rows = jnp.dot(metric_inv[0], fitted, precision=highest)
    coefficients = in_order(*xor_gather(coef_rows, "grid", 0), 0)
    coef_high, coef_low = split_rows(coefficients)
    coulomb_parts = jnp.dot(
        aux_block, jnp.stack([coef_high, coef_low], axis=1), preferred_element_type=jnp.float32
    )
    coulomb = coulomb_parts[:, 0] + coulomb_parts[:, 1]
    coulomb_total = jnp.sum(coefficients * weight_projection, axis=0, keepdims=True)
    potential = live_weight * (
        coulomb + exchange - coulomb_total / weight_sum - exchange_total / weight_sum
    )
    weighted_basis = (basis_rows * potential[:, None]).astype(jnp.bfloat16)
    half_rows = frag_basis // lax.axis_size("grid")
    left_first = lax.slice_in_dim(weighted_basis, 0, half_rows * lax.axis_size("grid"), axis=1)
    left_second = lax.dynamic_slice_in_dim(
        weighted_basis, frag_basis, half_rows * lax.axis_size("grid"), 1
    )
    first_first = contract(left_first, basis_rows[:, :frag_basis])
    first_second = contract(left_first, basis_rows[:, frag_basis:])
    second_second = contract(left_second, basis_rows[:, frag_basis:])
    diagonal, own_cross = paired_scatter(
        jnp.stack([first_first, second_second], axis=1), first_second, "grid"
    )
    own_first = diagonal[:, 0]
    own_second = diagonal[:, 1]
    groups = lax.axis_size("dimer")
    me = lax.axis_index("dimer")
    zero = jnp.zeros((), jnp.float32)

    def piece(dest):
        return jnp.where(dimer_pairs[0, 0] == dest, own_first, zero) + jnp.where(
            dimer_pairs[0, 1] == dest, own_second, zero
        )

    frag_fock = piece(me)
    for shift in range(1, groups):
        sent = piece(lax.rem(me + shift, groups))
        frag_fock = frag_fock + lax.ppermute(
            sent, "dimer", [(i, (i + shift) % groups) for i in range(groups)]
        )
    return (frag_fock[None], own_cross[None])


def solution(mesh):
    placed = (
        P("dimer", "grid", None),
        P("dimer", "grid", None),
        P("dimer", "grid", None),
        P(),
        P("dimer", None),
        P("dimer", "grid"),
        P("dimer", "grid"),
        P("dimer", "grid", None),
    )
    return jax.shard_map(
        shards,
        mesh=mesh,
        in_specs=placed,
        out_specs=(P("dimer", "grid", None), P("dimer", "grid", None)),
        check_vma=False,
    )
```

```python
import jax
import jax.numpy as jnp
from jax import lax
from jax.sharding import PartitionSpec as P

exchange_coeff = 0.9847450218426964


def split_rows(rows):
    high_part = rows.astype(jnp.bfloat16)
    high_back = lax.optimization_barrier(high_part).astype(jnp.float32)
    low_part = (rows - high_back).astype(jnp.bfloat16)
    return high_part, low_part


def contract(left_side, right_side):
    numbers = (((0,), (0,)), ((), ()))
    return lax.dot_general(left_side, right_side, numbers, preferred_element_type=jnp.float32)


def xor_sum(value, axis):
    size = lax.axis_size(axis)
    if size & (size - 1):
        return lax.psum(value, axis)
    step = 1
    while step < size:
        value = value + lax.ppermute(value, axis, [(i, i ^ step) for i in range(size)])
        step *= 2
    return value


def xor_gather(value, axis, dim):
    size = lax.axis_size(axis)
    if size & (size - 1):
        plain = jnp.arange(size, dtype=jnp.int32)
        return lax.all_gather(value, axis, axis=dim, tiled=True), plain, plain
    me = lax.axis_index(axis)
    bits = size.bit_length() - 1
    for bit in reversed(range(bits)):
        other = lax.ppermute(value, axis, [(i, i ^ (1 << bit)) for i in range(size)])
        value = jnp.concatenate([value, other], axis=dim)
    flip = [sum(((p >> b) & 1) << (bits - 1 - b) for b in range(bits)) for p in range(size)]
    flipped_me = sum(((me >> b) & 1) << (bits - 1 - b) for b in range(bits))
    table = jnp.array(flip, jnp.int32)
    return value, jnp.bitwise_xor(table, me), jnp.bitwise_xor(table, flipped_me)


def in_order(value, holder, place, dim):
    size = holder.shape[0]
    shape = value.shape
    blocks = value.reshape(shape[:dim] + (size, shape[dim] // size) + shape[dim + 1 :])
    return jnp.take(blocks, place, axis=dim).reshape(shape)


def scatter_chunks(value, axis):
    size = lax.axis_size(axis)
    return value.reshape((size, value.shape[0] // size) + value.shape[1:])


def scatter_step(value, axis, bit):
    size = lax.axis_size(axis)
    mine = (lax.axis_index(axis) >> bit) & 1
    pairs = value.reshape((value.shape[0] // 2, 2) + value.shape[1:])
    keep = lax.dynamic_index_in_dim(pairs, mine, axis=1, keepdims=False)
    send = lax.dynamic_index_in_dim(pairs, 1 - mine, axis=1, keepdims=False)
    return keep + lax.ppermute(send, axis, [(i, i ^ (1 << bit)) for i in range(size)])


def paired_scatter(lead, follow, axis):
    size = lax.axis_size(axis)
    if size & (size - 1):
        return (
            lax.psum_scatter(lead, axis, scatter_dimension=0, tiled=True),
            lax.psum_scatter(follow, axis, scatter_dimension=0, tiled=True),
        )
    lead = scatter_chunks(lead, axis)
    follow = scatter_chunks(follow, axis)
    bit = 0
    while (1 << bit) < size:
        lead = scatter_step(lead, axis, bit)
        follow, _ = lax.optimization_barrier((follow, lead))
        follow = scatter_step(follow, axis, bit)
        bit += 1
    return lead[0], follow[0]


def shards(basis_values, aux_values, factors, frag_slot, dimer_pairs, counts, weights, metric_inv):
    highest = lax.Precision.HIGHEST
    basis_rows = basis_values[0]
    aux_block = aux_values[0]
    points = basis_rows.shape[0]
    naux = aux_block.shape[1]
    frag_basis = basis_rows.shape[1] // 2
    live_count = counts[0, 0]
    position = lax.iota(jnp.int32, points)
    live_weight = jnp.where(position < live_count, weights[0], jnp.zeros((), jnp.float32))
    gathered, slot_held, _ = xor_gather(factors, "dimer", 0)
    frag_ids = lax.iota(jnp.int32, frag_slot.shape[0])
    wanted = jnp.sum(
        jnp.where(frag_ids[None, :] == dimer_pairs[0][:, None], frag_slot[None, :], 0), axis=1
    )
    selector = (slot_held[None, :] == wanted[:, None]).astype(jnp.bfloat16)
    chosen = jnp.einsum(
        "as,srk->ark", selector, gathered, preferred_element_type=jnp.float32
    ).astype(jnp.bfloat16)
    dimer_factors = in_order(*xor_gather(chosen, "grid", 1), 1)
    nocc = dimer_factors.shape[2]
    empty = jnp.zeros((frag_basis, nocc), jnp.bfloat16)
    block_factors = jnp.concatenate(
        [
            jnp.concatenate([dimer_factors[0], empty], axis=1),
            jnp.concatenate([empty, dimer_factors[1]], axis=1),
        ],
        axis=0,
    )
    orbitals = jnp.dot(basis_rows, block_factors, preferred_element_type=jnp.float32)
    density = jnp.sum(orbitals * orbitals, axis=1) / (2.0 * nocc)
    exchange = -exchange_coeff * jnp.cbrt(density)
    weighted_density = live_weight * density
    high_rows, low_rows = split_rows(jnp.stack([weighted_density, live_weight]))
    projections = jnp.dot(
        jnp.concatenate([high_rows, low_rows]), aux_block, preferred_element_type=jnp.float32
    )
    sums_part = jnp.stack([jnp.sum(live_weight * exchange), jnp.sum(live_weight)])
    first_lane = lax.broadcasted_iota(jnp.int32, (2, 128), 1) == 0
    payload = jnp.concatenate(
        [projections[:2] + projections[2:], jnp.where(first_lane, sums_part[:, None], 0.0)], axis=1
    )
    totals = xor_sum(payload, "grid")
    fitted = totals[0, :naux]
    weight_projection = totals[1, :naux]
    exchange_total = totals[0, naux]
    weight_sum = totals[1, naux]
    coef_rows = jnp.sum(metric_inv[0] * fitted[None, :], axis=1)
    coefficients = in_order(*xor_gather(coef_rows, "grid", 0), 0)
    coef_high, coef_low = split_rows(coefficients)
    coulomb_parts = jnp.dot(
        aux_block, jnp.stack([coef_high, coef_low], axis=1), preferred_element_type=jnp.float32
    )
    coulomb = coulomb_parts[:, 0] + coulomb_parts[:, 1]
    potential_total = jnp.dot(coefficients, weight_projection, precision=highest) + exchange_total
    average = potential_total / weight_sum
    potential = live_weight * (coulomb + exchange - average)
    weighted_basis = (basis_rows * potential[:, None]).astype(jnp.bfloat16)
    half_rows = frag_basis // lax.axis_size("grid")
    left_first = lax.slice_in_dim(weighted_basis, 0, half_rows * lax.axis_size("grid"), axis=1)
    left_second = lax.dynamic_slice_in_dim(
        weighted_basis, frag_basis, half_rows * lax.axis_size("grid"), 1
    )
    first_first = contract(left_first, basis_rows[:, :frag_basis])
    first_second = contract(left_first, basis_rows[:, frag_basis:])
    second_second = contract(left_second, basis_rows[:, frag_basis:])
    diagonal, own_cross = paired_scatter(
        jnp.stack([first_first, second_second], axis=1), first_second, "grid"
    )
    own_first = diagonal[:, 0]
    own_second = diagonal[:, 1]
    groups = lax.axis_size("dimer")
    me = lax.axis_index("dimer")
    zero = jnp.zeros((), jnp.float32)

    def piece(dest):
        return jnp.where(dimer_pairs[0, 0] == dest, own_first, zero) + jnp.where(
            dimer_pairs[0, 1] == dest, own_second, zero
        )

    frag_fock = piece(me)
    paired = groups & (groups - 1) == 0
    for shift in range(1, groups):
        if paired:
            dest, pairs = jnp.bitwise_xor(me, shift), [(i, i ^ shift) for i in range(groups)]
        else:
            dest, pairs = lax.rem(me + shift, groups), [(i, (i + shift) % groups) for i in range(groups)]
        frag_fock = frag_fock + lax.ppermute(piece(dest), "dimer", pairs)
    return (frag_fock[None], own_cross[None])


def solution(mesh):
    placed = (
        P("dimer", "grid", None),
        P("dimer", "grid", None),
        P("dimer", "grid", None),
        P(),
        P("dimer", None),
        P("dimer", "grid"),
        P("dimer", "grid"),
        P("dimer", "grid", None),
    )
    return jax.shard_map(
        shards,
        mesh=mesh,
        in_specs=placed,
        out_specs=(P("dimer", "grid", None), P("dimer", "grid", None)),
        check_vma=False,
    )
```

```python
import jax
import jax.numpy as jnp
from jax import lax
from jax.sharding import PartitionSpec as P

exchange_coeff = 0.9847450218426964


def split_rows(rows):
    high_part = rows.astype(jnp.bfloat16)
    high_back = lax.optimization_barrier(high_part).astype(jnp.float32)
    low_part = (rows - high_back).astype(jnp.bfloat16)
    return high_part, low_part


def contract(left_side, right_side):
    numbers = (((0,), (0,)), ((), ()))
    return lax.dot_general(left_side, right_side, numbers, preferred_element_type=jnp.float32)


def xor_sum(value, axis):
    size = lax.axis_size(axis)
    if size & (size - 1):
        return lax.psum(value, axis)
    step = 1
    while step < size:
        value = value + lax.ppermute(value, axis, [(i, i ^ step) for i in range(size)])
        step *= 2
    return value


def xor_gather(value, axis, dim):
    size = lax.axis_size(axis)
    if size & (size - 1):
        plain = jnp.arange(size, dtype=jnp.int32)
        return lax.all_gather(value, axis, axis=dim, tiled=True), plain, plain
    me = lax.axis_index(axis)
    bits = size.bit_length() - 1
    for bit in reversed(range(bits)):
        other = lax.ppermute(value, axis, [(i, i ^ (1 << bit)) for i in range(size)])
        value = jnp.concatenate([value, other], axis=dim)
    flip = [sum(((p >> b) & 1) << (bits - 1 - b) for b in range(bits)) for p in range(size)]
    flipped_me = sum(((me >> b) & 1) << (bits - 1 - b) for b in range(bits))
    table = jnp.array(flip, jnp.int32)
    return value, jnp.bitwise_xor(table, me), jnp.bitwise_xor(table, flipped_me)


def in_order(value, holder, place, dim):
    size = holder.shape[0]
    shape = value.shape
    blocks = value.reshape(shape[:dim] + (size, shape[dim] // size) + shape[dim + 1 :])
    return jnp.take(blocks, place, axis=dim).reshape(shape)


def scatter_chunks(value, axis):
    size = lax.axis_size(axis)
    return value.reshape((size, value.shape[0] // size) + value.shape[1:])


def scatter_step(value, axis, bit):
    size = lax.axis_size(axis)
    mine = (lax.axis_index(axis) >> bit) & 1
    pairs = value.reshape((value.shape[0] // 2, 2) + value.shape[1:])
    keep = lax.dynamic_index_in_dim(pairs, mine, axis=1, keepdims=False)
    send = lax.dynamic_index_in_dim(pairs, 1 - mine, axis=1, keepdims=False)
    return keep + lax.ppermute(send, axis, [(i, i ^ (1 << bit)) for i in range(size)])


def paired_scatter(lead, follow, axis):
    size = lax.axis_size(axis)
    if size & (size - 1):
        return (
            lax.psum_scatter(lead, axis, scatter_dimension=0, tiled=True),
            lax.psum_scatter(follow, axis, scatter_dimension=0, tiled=True),
        )
    lead = scatter_chunks(lead, axis)
    follow = scatter_chunks(follow, axis)
    bit = 0
    while (1 << bit) < size:
        lead = scatter_step(lead, axis, bit)
        follow, _ = lax.optimization_barrier((follow, lead))
        follow = scatter_step(follow, axis, bit)
        bit += 1
    return lead[0], follow[0]


def shards(basis_values, aux_values, factors, frag_slot, dimer_pairs, counts, weights, metric_inv):
    highest = lax.Precision.HIGHEST
    basis_rows = basis_values[0]
    aux_block = aux_values[0]
    points = basis_rows.shape[0]
    naux = aux_block.shape[1]
    frag_basis = basis_rows.shape[1] // 2
    live_count = counts[0, 0]
    position = lax.iota(jnp.int32, points)
    live_weight = jnp.where(position < live_count, weights[0], jnp.zeros((), jnp.float32))
    gathered, slot_held, _ = xor_gather(factors, "dimer", 0)
    frag_ids = lax.iota(jnp.int32, frag_slot.shape[0])
    wanted = jnp.sum(
        jnp.where(frag_ids[None, :] == dimer_pairs[0][:, None], frag_slot[None, :], 0), axis=1
    )
    selector = (slot_held[None, :] == wanted[:, None]).astype(jnp.bfloat16)
    chosen = jnp.einsum(
        "as,srk->ark", selector, gathered, preferred_element_type=jnp.float32
    ).astype(jnp.bfloat16)
    dimer_factors = in_order(*xor_gather(chosen, "grid", 1), 1)
    nocc = dimer_factors.shape[2]
    empty = jnp.zeros((frag_basis, nocc), jnp.bfloat16)
    block_factors = jnp.concatenate(
        [
            jnp.concatenate([dimer_factors[0], empty], axis=1),
            jnp.concatenate([empty, dimer_factors[1]], axis=1),
        ],
        axis=0,
    )
    orbitals = jnp.dot(basis_rows, block_factors, preferred_element_type=jnp.float32)
    density = jnp.sum(orbitals * orbitals, axis=1) / (2.0 * nocc)
    exchange = -exchange_coeff * jnp.cbrt(density)
    weighted_density = live_weight * density
    high_rows, low_rows = split_rows(jnp.stack([weighted_density, live_weight]))
    projections = jnp.dot(
        jnp.concatenate([high_rows, low_rows]), aux_block, preferred_element_type=jnp.float32
    )
    sums_part = jnp.stack([jnp.sum(live_weight * exchange), jnp.sum(live_weight)])
    first_lane = lax.broadcasted_iota(jnp.int32, (2, 128), 1) == 0
    payload = jnp.concatenate(
        [projections[:2] + projections[2:], jnp.where(first_lane, sums_part[:, None], 0.0)], axis=1
    )
    totals = xor_sum(payload, "grid")
    fitted = totals[0, :naux]
    weight_projection = totals[1, :naux]
    exchange_total = totals[0, naux]
    weight_sum = totals[1, naux]
    coef_rows = jnp.sum(metric_inv[0] * fitted[None, :], axis=1)
    coefficients = in_order(*xor_gather(coef_rows, "grid", 0), 0)
    coulomb = jnp.sum(aux_block.astype(jnp.float32) * coefficients[None, :], axis=1)
    potential_total = jnp.dot(coefficients, weight_projection, precision=highest) + exchange_total
    average = potential_total / weight_sum
    potential = live_weight * (coulomb + exchange - average)
    weighted_basis = (basis_rows * potential[:, None]).astype(jnp.bfloat16)
    half_rows = frag_basis // lax.axis_size("grid")
    left_first = lax.slice_in_dim(weighted_basis, 0, half_rows * lax.axis_size("grid"), axis=1)
    left_second = lax.dynamic_slice_in_dim(
        weighted_basis, frag_basis, half_rows * lax.axis_size("grid"), 1
    )
    first_first = contract(left_first, basis_rows[:, :frag_basis])
    first_second = contract(left_first, basis_rows[:, frag_basis:])
    second_second = contract(left_second, basis_rows[:, frag_basis:])
    diagonal, own_cross = paired_scatter(
        jnp.stack([first_first, second_second], axis=1), first_second, "grid"
    )
    own_first = diagonal[:, 0]
    own_second = diagonal[:, 1]
    groups = lax.axis_size("dimer")
    me = lax.axis_index("dimer")
    zero = jnp.zeros((), jnp.float32)

    def piece(dest):
        return jnp.where(dimer_pairs[0, 0] == dest, own_first, zero) + jnp.where(
            dimer_pairs[0, 1] == dest, own_second, zero
        )

    frag_fock = piece(me)
    paired = groups & (groups - 1) == 0
    for shift in range(1, groups):
        if paired:
            dest, pairs = jnp.bitwise_xor(me, shift), [(i, i ^ shift) for i in range(groups)]
        else:
            dest, pairs = lax.rem(me + shift, groups), [(i, (i + shift) % groups) for i in range(groups)]
        frag_fock = frag_fock + lax.ppermute(piece(dest), "dimer", pairs)
    return (frag_fock[None], own_cross[None])


def solution(mesh):
    placed = (
        P("dimer", "grid", None),
        P("dimer", "grid", None),
        P("dimer", "grid", None),
        P(),
        P("dimer", None),
        P("dimer", "grid"),
        P("dimer", "grid"),
        P("dimer", "grid", None),
    )
    return jax.shard_map(
        shards,
        mesh=mesh,
        in_specs=placed,
        out_specs=(P("dimer", "grid", None), P("dimer", "grid", None)),
        check_vma=False,
    )
```

```python
import jax
import jax.numpy as jnp
from jax import lax
from jax.sharding import PartitionSpec as P

exchange_coeff = 0.9847450218426964


def split_rows(rows):
    high_part = rows.astype(jnp.bfloat16)
    high_back = lax.optimization_barrier(high_part).astype(jnp.float32)
    low_part = (rows - high_back).astype(jnp.bfloat16)
    return high_part, low_part


def contract(left_side, right_side):
    numbers = (((0,), (0,)), ((), ()))
    return lax.dot_general(left_side, right_side, numbers, preferred_element_type=jnp.float32)


def xor_sum(value, axis):
    size = lax.axis_size(axis)
    if size & (size - 1):
        return lax.psum(value, axis)
    step = 1
    while step < size:
        value = value + lax.ppermute(value, axis, [(i, i ^ step) for i in range(size)])
        step *= 2
    return value


def xor_gather(value, axis, dim):
    size = lax.axis_size(axis)
    if size & (size - 1):
        plain = jnp.arange(size, dtype=jnp.int32)
        return lax.all_gather(value, axis, axis=dim, tiled=True), plain, plain
    me = lax.axis_index(axis)
    bits = size.bit_length() - 1
    for bit in reversed(range(bits)):
        other = lax.ppermute(value, axis, [(i, i ^ (1 << bit)) for i in range(size)])
        value = jnp.concatenate([value, other], axis=dim)
    flip = [sum(((p >> b) & 1) << (bits - 1 - b) for b in range(bits)) for p in range(size)]
    flipped_me = sum(((me >> b) & 1) << (bits - 1 - b) for b in range(bits))
    table = jnp.array(flip, jnp.int32)
    return value, jnp.bitwise_xor(table, me), jnp.bitwise_xor(table, flipped_me)


def in_order(value, holder, place, dim):
    size = holder.shape[0]
    shape = value.shape
    blocks = value.reshape(shape[:dim] + (size, shape[dim] // size) + shape[dim + 1 :])
    return jnp.take(blocks, place, axis=dim).reshape(shape)


def scatter_chunks(value, axis):
    size = lax.axis_size(axis)
    return value.reshape((size, value.shape[0] // size) + value.shape[1:])


def scatter_step(value, axis, bit):
    size = lax.axis_size(axis)
    mine = (lax.axis_index(axis) >> bit) & 1
    pairs = value.reshape((value.shape[0] // 2, 2) + value.shape[1:])
    keep = lax.dynamic_index_in_dim(pairs, mine, axis=1, keepdims=False)
    send = lax.dynamic_index_in_dim(pairs, 1 - mine, axis=1, keepdims=False)
    return keep + lax.ppermute(send, axis, [(i, i ^ (1 << bit)) for i in range(size)])


def paired_scatter(lead, follow, axis):
    size = lax.axis_size(axis)
    if size & (size - 1):
        return (
            lax.psum_scatter(lead, axis, scatter_dimension=0, tiled=True),
            lax.psum_scatter(follow, axis, scatter_dimension=0, tiled=True),
        )
    lead = scatter_chunks(lead, axis)
    follow = scatter_chunks(follow, axis)
    bit = 0
    while (1 << bit) < size:
        lead = scatter_step(lead, axis, bit)
        follow, _ = lax.optimization_barrier((follow, lead))
        follow = scatter_step(follow, axis, bit)
        bit += 1
    return lead[0], follow[0]


def shards(basis_values, aux_values, factors, frag_slot, dimer_pairs, counts, weights, metric_inv):
    highest = lax.Precision.HIGHEST
    basis_rows = basis_values[0]
    aux_block = aux_values[0]
    points = basis_rows.shape[0]
    naux = aux_block.shape[1]
    frag_basis = basis_rows.shape[1] // 2
    live_count = counts[0, 0]
    position = lax.iota(jnp.int32, points)
    live_weight = jnp.where(position < live_count, weights[0], jnp.zeros((), jnp.float32))
    gathered, slot_held, _ = xor_gather(factors, "dimer", 0)
    frag_ids = lax.iota(jnp.int32, frag_slot.shape[0])
    wanted = jnp.sum(
        jnp.where(frag_ids[None, :] == dimer_pairs[0][:, None], frag_slot[None, :], 0), axis=1
    )
    chosen = jnp.stack(
        [
            jnp.sum(
                jnp.where(
                    (slot_held == wanted[a])[:, None, None], gathered, jnp.zeros((), gathered.dtype)
                ),
                axis=0,
            )
            for a in range(2)
        ]
    )
    dimer_factors = in_order(*xor_gather(chosen, "grid", 1), 1)
    nocc = dimer_factors.shape[2]
    empty = jnp.zeros((frag_basis, nocc), jnp.bfloat16)
    block_factors = jnp.concatenate(
        [
            jnp.concatenate([dimer_factors[0], empty], axis=1),
            jnp.concatenate([empty, dimer_factors[1]], axis=1),
        ],
        axis=0,
    )
    orbitals = jnp.dot(basis_rows, block_factors, preferred_element_type=jnp.float32)
    density = jnp.sum(orbitals * orbitals, axis=1) / (2.0 * nocc)
    exchange = -exchange_coeff * jnp.cbrt(density)
    weighted_density = live_weight * density
    high_rows, low_rows = split_rows(jnp.stack([weighted_density, live_weight]))
    projections = jnp.dot(
        jnp.concatenate([high_rows, low_rows]), aux_block, preferred_element_type=jnp.float32
    )
    sums_part = jnp.stack([jnp.sum(live_weight * exchange), jnp.sum(live_weight)])
    first_lane = lax.broadcasted_iota(jnp.int32, (2, 128), 1) == 0
    payload = jnp.concatenate(
        [projections[:2] + projections[2:], jnp.where(first_lane, sums_part[:, None], 0.0)], axis=1
    )
    totals = xor_sum(payload, "grid")
    fitted = totals[0, :naux]
    weight_projection = totals[1, :naux]
    exchange_total = totals[0, naux]
    weight_sum = totals[1, naux]
    coef_rows = jnp.sum(metric_inv[0] * fitted[None, :], axis=1)
    coefficients = in_order(*xor_gather(coef_rows, "grid", 0), 0)
    coulomb = jnp.sum(aux_block.astype(jnp.float32) * coefficients[None, :], axis=1)
    potential_total = jnp.sum(coefficients * weight_projection) + exchange_total
    average = potential_total / weight_sum
    potential = live_weight * (coulomb + exchange - average)
    weighted_basis = (basis_rows * potential[:, None]).astype(jnp.bfloat16)
    half_rows = frag_basis // lax.axis_size("grid")
    left_first = lax.slice_in_dim(weighted_basis, 0, half_rows * lax.axis_size("grid"), axis=1)
    left_second = lax.dynamic_slice_in_dim(
        weighted_basis, frag_basis, half_rows * lax.axis_size("grid"), 1
    )
    first_first = contract(left_first, basis_rows[:, :frag_basis])
    first_second = contract(left_first, basis_rows[:, frag_basis:])
    second_second = contract(left_second, basis_rows[:, frag_basis:])
    diagonal, own_cross = paired_scatter(
        jnp.stack([first_first, second_second], axis=1), first_second, "grid"
    )
    own_first = diagonal[:, 0]
    own_second = diagonal[:, 1]
    groups = lax.axis_size("dimer")
    me = lax.axis_index("dimer")
    zero = jnp.zeros((), jnp.float32)

    def piece(dest):
        return jnp.where(dimer_pairs[0, 0] == dest, own_first, zero) + jnp.where(
            dimer_pairs[0, 1] == dest, own_second, zero
        )

    frag_fock = piece(me)
    paired = groups & (groups - 1) == 0
    for shift in range(1, groups):
        if paired:
            dest, pairs = jnp.bitwise_xor(me, shift), [(i, i ^ shift) for i in range(groups)]
        else:
            dest, pairs = lax.rem(me + shift, groups), [(i, (i + shift) % groups) for i in range(groups)]
        frag_fock = frag_fock + lax.ppermute(piece(dest), "dimer", pairs)
    return (frag_fock[None], own_cross[None])


def solution(mesh):
    placed = (
        P("dimer", "grid", None),
        P("dimer", "grid", None),
        P("dimer", "grid", None),
        P(),
        P("dimer", None),
        P("dimer", "grid"),
        P("dimer", "grid"),
        P("dimer", "grid", None),
    )
    return jax.shard_map(
        shards,
        mesh=mesh,
        in_specs=placed,
        out_specs=(P("dimer", "grid", None), P("dimer", "grid", None)),
        check_vma=False,
    )
```

```python
import jax
import jax.numpy as jnp
from jax import lax
from jax.sharding import PartitionSpec as P

exchange_coeff = 0.9847450218426964


def split_rows(rows):
    high_part = rows.astype(jnp.bfloat16)
    high_back = lax.optimization_barrier(high_part).astype(jnp.float32)
    low_part = (rows - high_back).astype(jnp.bfloat16)
    return high_part, low_part


def contract(left_side, right_side):
    numbers = (((0,), (0,)), ((), ()))
    return lax.dot_general(left_side, right_side, numbers, preferred_element_type=jnp.float32)


def xor_sum(value, axis):
    size = lax.axis_size(axis)
    if size & (size - 1):
        return lax.psum(value, axis)
    step = 1
    while step < size:
        value = value + lax.ppermute(value, axis, [(i, i ^ step) for i in range(size)])
        step *= 2
    return value


def xor_gather(value, axis, dim):
    size = lax.axis_size(axis)
    if size & (size - 1):
        plain = jnp.arange(size, dtype=jnp.int32)
        return lax.all_gather(value, axis, axis=dim, tiled=True), plain, plain
    me = lax.axis_index(axis)
    bits = size.bit_length() - 1
    for bit in reversed(range(bits)):
        other = lax.ppermute(value, axis, [(i, i ^ (1 << bit)) for i in range(size)])
        value = jnp.concatenate([value, other], axis=dim)
    flip = [sum(((p >> b) & 1) << (bits - 1 - b) for b in range(bits)) for p in range(size)]
    flipped_me = sum(((me >> b) & 1) << (bits - 1 - b) for b in range(bits))
    table = jnp.array(flip, jnp.int32)
    return value, jnp.bitwise_xor(table, me), jnp.bitwise_xor(table, flipped_me)


def in_order(value, holder, place, dim):
    size = holder.shape[0]
    shape = value.shape
    blocks = value.reshape(shape[:dim] + (size, shape[dim] // size) + shape[dim + 1 :])
    return jnp.take(blocks, place, axis=dim).reshape(shape)


def scatter_chunks(value, axis):
    size = lax.axis_size(axis)
    return value.reshape((size, value.shape[0] // size) + value.shape[1:])


def scatter_step(value, axis, bit):
    size = lax.axis_size(axis)
    mine = (lax.axis_index(axis) >> bit) & 1
    pairs = value.reshape((value.shape[0] // 2, 2) + value.shape[1:])
    keep = lax.dynamic_index_in_dim(pairs, mine, axis=1, keepdims=False)
    send = lax.dynamic_index_in_dim(pairs, 1 - mine, axis=1, keepdims=False)
    return keep + lax.ppermute(send, axis, [(i, i ^ (1 << bit)) for i in range(size)])


def paired_scatter(lead, follow, axis):
    size = lax.axis_size(axis)
    if size & (size - 1):
        return (
            lax.psum_scatter(lead, axis, scatter_dimension=0, tiled=True),
            lax.psum_scatter(follow, axis, scatter_dimension=0, tiled=True),
        )
    lead = scatter_chunks(lead, axis)
    follow = scatter_chunks(follow, axis)
    bit = 0
    while (1 << bit) < size:
        lead = scatter_step(lead, axis, bit)
        follow, _ = lax.optimization_barrier((follow, lead))
        follow = scatter_step(follow, axis, bit)
        bit += 1
    return lead[0], follow[0]


def shards(basis_values, aux_values, factors, frag_slot, dimer_pairs, counts, weights, metric_inv):
    highest = lax.Precision.HIGHEST
    basis_rows = basis_values[0]
    aux_block = aux_values[0]
    points = basis_rows.shape[0]
    naux = aux_block.shape[1]
    frag_basis = basis_rows.shape[1] // 2
    live_count = counts[0, 0]
    position = lax.iota(jnp.int32, points)
    live_weight = jnp.where(position < live_count, weights[0], jnp.zeros((), jnp.float32))
    gathered, slot_held, _ = xor_gather(factors, "dimer", 0)
    frag_ids = lax.iota(jnp.int32, frag_slot.shape[0])
    wanted = jnp.sum(
        jnp.where(frag_ids[None, :] == dimer_pairs[0][:, None], frag_slot[None, :], 0), axis=1
    )
    selector = (slot_held[None, :] == wanted[:, None]).astype(jnp.bfloat16)
    chosen = jnp.einsum(
        "as,srk->ark", selector, gathered, preferred_element_type=jnp.float32
    ).astype(jnp.bfloat16)
    dimer_factors = in_order(*xor_gather(chosen, "grid", 1), 1)
    nocc = dimer_factors.shape[2]
    empty = jnp.zeros((frag_basis, nocc), jnp.bfloat16)
    block_factors = jnp.concatenate(
        [
            jnp.concatenate([dimer_factors[0], empty], axis=1),
            jnp.concatenate([empty, dimer_factors[1]], axis=1),
        ],
        axis=0,
    )
    orbitals = jnp.dot(basis_rows, block_factors, preferred_element_type=jnp.float32)
    density = jnp.sum(orbitals * orbitals, axis=1) / (2.0 * nocc)
    exchange = -exchange_coeff * jnp.cbrt(density)
    weighted_density = live_weight * density
    high_rows, low_rows = split_rows(jnp.stack([weighted_density, live_weight]))
    projections = jnp.dot(
        jnp.concatenate([high_rows, low_rows]), aux_block, preferred_element_type=jnp.float32
    )
    sums_part = jnp.stack([jnp.sum(live_weight * exchange), jnp.sum(live_weight)])
    first_lane = lax.broadcasted_iota(jnp.int32, (2, 128), 1) == 0
    payload = jnp.concatenate(
        [projections[:2] + projections[2:], jnp.where(first_lane, sums_part[:, None], 0.0)], axis=1
    )
    totals = xor_sum(payload, "grid")
    fitted = totals[0, :naux]
    weight_projection = totals[1, :naux]
    exchange_total = totals[0, naux : naux + 1]
    weight_sum = totals[1, naux : naux + 1]
    coef_rows = jnp.sum(metric_inv[0] * fitted[None, :], axis=1)
    coefficients = in_order(*xor_gather(coef_rows, "grid", 0), 0)
    coulomb = jnp.sum(aux_block.astype(jnp.float32) * coefficients[None, :], axis=1)
    coulomb_total = jnp.sum(coefficients * weight_projection, axis=0, keepdims=True)
    potential = live_weight * (
        coulomb + exchange - coulomb_total / weight_sum - exchange_total / weight_sum
    )
    weighted_basis = (basis_rows * potential[:, None]).astype(jnp.bfloat16)
    half_rows = frag_basis // lax.axis_size("grid")
    left_first = lax.slice_in_dim(weighted_basis, 0, half_rows * lax.axis_size("grid"), axis=1)
    left_second = lax.dynamic_slice_in_dim(
        weighted_basis, frag_basis, half_rows * lax.axis_size("grid"), 1
    )
    first_first = contract(left_first, basis_rows[:, :frag_basis])
    first_second = contract(left_first, basis_rows[:, frag_basis:])
    second_second = contract(left_second, basis_rows[:, frag_basis:])
    diagonal, own_cross = paired_scatter(
        jnp.stack([first_first, second_second], axis=1), first_second, "grid"
    )
    own_first = diagonal[:, 0]
    own_second = diagonal[:, 1]
    groups = lax.axis_size("dimer")
    me = lax.axis_index("dimer")
    zero = jnp.zeros((), jnp.float32)

    def piece(dest):
        return jnp.where(dimer_pairs[0, 0] == dest, own_first, zero) + jnp.where(
            dimer_pairs[0, 1] == dest, own_second, zero
        )

    frag_fock = piece(me)
    paired = groups & (groups - 1) == 0
    for shift in range(1, groups):
        if paired:
            dest, pairs = jnp.bitwise_xor(me, shift), [(i, i ^ shift) for i in range(groups)]
        else:
            dest, pairs = lax.rem(me + shift, groups), [(i, (i + shift) % groups) for i in range(groups)]
        frag_fock = frag_fock + lax.ppermute(piece(dest), "dimer", pairs)
    return (frag_fock[None], own_cross[None])


def solution(mesh):
    placed = (
        P("dimer", "grid", None),
        P("dimer", "grid", None),
        P("dimer", "grid", None),
        P(),
        P("dimer", None),
        P("dimer", "grid"),
        P("dimer", "grid"),
        P("dimer", "grid", None),
    )
    return jax.shard_map(
        shards,
        mesh=mesh,
        in_specs=placed,
        out_specs=(P("dimer", "grid", None), P("dimer", "grid", None)),
        check_vma=False,
    )
```

```python
import jax
import jax.numpy as jnp
from jax import lax
from jax.sharding import PartitionSpec as P

exchange_coeff = 0.9847450218426964


def split_rows(rows):
    high_part = rows.astype(jnp.bfloat16)
    high_back = lax.optimization_barrier(high_part).astype(jnp.float32)
    low_part = (rows - high_back).astype(jnp.bfloat16)
    return high_part, low_part


def contract(left_side, right_side):
    numbers = (((0,), (0,)), ((), ()))
    return lax.dot_general(left_side, right_side, numbers, preferred_element_type=jnp.float32)


def xor_sum(value, axis):
    size = lax.axis_size(axis)
    if size & (size - 1):
        return lax.psum(value, axis)
    step = 1
    while step < size:
        value = value + lax.ppermute(value, axis, [(i, i ^ step) for i in range(size)])
        step *= 2
    return value


def xor_gather(value, axis, dim):
    size = lax.axis_size(axis)
    if size & (size - 1):
        plain = jnp.arange(size, dtype=jnp.int32)
        return lax.all_gather(value, axis, axis=dim, tiled=True), plain, plain
    me = lax.axis_index(axis)
    bits = size.bit_length() - 1
    for bit in reversed(range(bits)):
        other = lax.ppermute(value, axis, [(i, i ^ (1 << bit)) for i in range(size)])
        value = jnp.concatenate([value, other], axis=dim)
    flip = [sum(((p >> b) & 1) << (bits - 1 - b) for b in range(bits)) for p in range(size)]
    flipped_me = sum(((me >> b) & 1) << (bits - 1 - b) for b in range(bits))
    table = jnp.array(flip, jnp.int32)
    return value, jnp.bitwise_xor(table, me), jnp.bitwise_xor(table, flipped_me)


def in_order(value, holder, place, dim):
    size = holder.shape[0]
    shape = value.shape
    blocks = value.reshape(shape[:dim] + (size, shape[dim] // size) + shape[dim + 1 :])
    return jnp.take(blocks, place, axis=dim).reshape(shape)


def scatter_chunks(value, axis):
    size = lax.axis_size(axis)
    return value.reshape((size, value.shape[0] // size) + value.shape[1:])


def scatter_step(value, axis, bit):
    size = lax.axis_size(axis)
    mine = (lax.axis_index(axis) >> bit) & 1
    pairs = value.reshape((value.shape[0] // 2, 2) + value.shape[1:])
    keep = lax.dynamic_index_in_dim(pairs, mine, axis=1, keepdims=False)
    send = lax.dynamic_index_in_dim(pairs, 1 - mine, axis=1, keepdims=False)
    return keep + lax.ppermute(send, axis, [(i, i ^ (1 << bit)) for i in range(size)])


def paired_scatter(lead, follow, axis):
    size = lax.axis_size(axis)
    if size & (size - 1):
        return (
            lax.psum_scatter(lead, axis, scatter_dimension=0, tiled=True),
            lax.psum_scatter(follow, axis, scatter_dimension=0, tiled=True),
        )
    lead = scatter_chunks(lead, axis)
    follow = scatter_chunks(follow, axis)
    bit = 0
    while (1 << bit) < size:
        lead = scatter_step(lead, axis, bit)
        follow, _ = lax.optimization_barrier((follow, lead))
        follow = scatter_step(follow, axis, bit)
        bit += 1
    return lead[0], follow[0]


def shards(basis_values, aux_values, factors, frag_slot, dimer_pairs, counts, weights, metric_inv):
    highest = lax.Precision.HIGHEST
    basis_rows = basis_values[0]
    aux_block = aux_values[0]
    points = basis_rows.shape[0]
    naux = aux_block.shape[1]
    frag_basis = basis_rows.shape[1] // 2
    live_count = counts[0, 0]
    position = lax.iota(jnp.int32, points)
    live_weight = jnp.where(position < live_count, weights[0], jnp.zeros((), jnp.float32))
    gathered, slot_held, _ = xor_gather(factors, "dimer", 0)
    frag_ids = lax.iota(jnp.int32, frag_slot.shape[0])
    wanted = jnp.sum(
        jnp.where(frag_ids[None, :] == dimer_pairs[0][:, None], frag_slot[None, :], 0), axis=1
    )
    selector = (slot_held[None, :] == wanted[:, None]).astype(jnp.bfloat16)
    chosen = jnp.einsum(
        "as,srk->ark", selector, gathered, preferred_element_type=jnp.float32
    ).astype(jnp.bfloat16)
    dimer_factors = in_order(*xor_gather(chosen, "grid", 1), 1)
    nocc = dimer_factors.shape[2]
    empty = jnp.zeros((frag_basis, nocc), jnp.bfloat16)
    block_factors = jnp.concatenate(
        [
            jnp.concatenate([dimer_factors[0], empty], axis=1),
            jnp.concatenate([empty, dimer_factors[1]], axis=1),
        ],
        axis=0,
    )
    orbitals = jnp.dot(basis_rows, block_factors, preferred_element_type=jnp.float32)
    density = jnp.sum(orbitals * orbitals, axis=1) / (2.0 * nocc)
    exchange = -exchange_coeff * jnp.cbrt(density)
    weighted_density = live_weight * density
    high_rows, low_rows = split_rows(jnp.stack([weighted_density, live_weight]))
    projections = jnp.dot(
        jnp.concatenate([high_rows, low_rows]), aux_block, preferred_element_type=jnp.float32
    )
    weight_total = lax.optimization_barrier(jnp.sum(live_weight))
    sums_part = jnp.stack([jnp.sum(live_weight * exchange), weight_total])
    first_lane = lax.broadcasted_iota(jnp.int32, (2, 128), 1) == 0
    payload = jnp.concatenate(
        [projections[:2] + projections[2:], jnp.where(first_lane, sums_part[:, None], 0.0)], axis=1
    )
    totals = xor_sum(payload, "grid")
    fitted = totals[0, :naux]
    weight_projection = totals[1, :naux]
    exchange_total = totals[0, naux]
    weight_sum = totals[1, naux]
    coef_rows = jnp.sum(metric_inv[0] * fitted[None, :], axis=1)
    coefficients = in_order(*xor_gather(coef_rows, "grid", 0), 0)
    coulomb = jnp.sum(aux_block.astype(jnp.float32) * coefficients[None, :], axis=1)
    potential_total = jnp.dot(coefficients, weight_projection, precision=highest) + exchange_total
    average = potential_total / weight_sum
    potential = live_weight * (coulomb + exchange - average)
    weighted_basis = (basis_rows * potential[:, None]).astype(jnp.bfloat16)
    half_rows = frag_basis // lax.axis_size("grid")
    left_first = lax.slice_in_dim(weighted_basis, 0, half_rows * lax.axis_size("grid"), axis=1)
    left_second = lax.dynamic_slice_in_dim(
        weighted_basis, frag_basis, half_rows * lax.axis_size("grid"), 1
    )
    first_first = contract(left_first, basis_rows[:, :frag_basis])
    first_second = contract(left_first, basis_rows[:, frag_basis:])
    second_second = contract(left_second, basis_rows[:, frag_basis:])
    diagonal, own_cross = paired_scatter(
        jnp.stack([first_first, second_second], axis=1), first_second, "grid"
    )
    own_first = diagonal[:, 0]
    own_second = diagonal[:, 1]
    groups = lax.axis_size("dimer")
    me = lax.axis_index("dimer")
    zero = jnp.zeros((), jnp.float32)

    def piece(dest):
        return jnp.where(dimer_pairs[0, 0] == dest, own_first, zero) + jnp.where(
            dimer_pairs[0, 1] == dest, own_second, zero
        )

    frag_fock = piece(me)
    paired = groups & (groups - 1) == 0
    for shift in range(1, groups):
        if paired:
            dest, pairs = jnp.bitwise_xor(me, shift), [(i, i ^ shift) for i in range(groups)]
        else:
            dest, pairs = lax.rem(me + shift, groups), [(i, (i + shift) % groups) for i in range(groups)]
        frag_fock = frag_fock + lax.ppermute(piece(dest), "dimer", pairs)
    return (frag_fock[None], own_cross[None])


def solution(mesh):
    placed = (
        P("dimer", "grid", None),
        P("dimer", "grid", None),
        P("dimer", "grid", None),
        P(),
        P("dimer", None),
        P("dimer", "grid"),
        P("dimer", "grid"),
        P("dimer", "grid", None),
    )
    return jax.shard_map(
        shards,
        mesh=mesh,
        in_specs=placed,
        out_specs=(P("dimer", "grid", None), P("dimer", "grid", None)),
        check_vma=False,
    )
```

```python
import jax
import jax.numpy as jnp
from jax import lax
from jax.sharding import PartitionSpec as P

exchange_coeff = 0.9847450218426964


def split_rows(rows):
    high_part = rows.astype(jnp.bfloat16)
    high_back = lax.optimization_barrier(high_part).astype(jnp.float32)
    low_part = (rows - high_back).astype(jnp.bfloat16)
    return high_part, low_part


def contract(left_side, right_side):
    numbers = (((0,), (0,)), ((), ()))
    return lax.dot_general(left_side, right_side, numbers, preferred_element_type=jnp.float32)


def xor_sum(value, axis):
    size = lax.axis_size(axis)
    if size & (size - 1):
        return lax.psum(value, axis)
    step = size // 2
    while step:
        value = value + lax.ppermute(value, axis, [(i, i ^ step) for i in range(size)])
        step //= 2
    return value


def xor_gather(value, axis, dim):
    size = lax.axis_size(axis)
    if size & (size - 1):
        plain = jnp.arange(size, dtype=jnp.int32)
        return lax.all_gather(value, axis, axis=dim, tiled=True), plain, plain
    me = lax.axis_index(axis)
    bits = size.bit_length() - 1
    for bit in reversed(range(bits)):
        other = lax.ppermute(value, axis, [(i, i ^ (1 << bit)) for i in range(size)])
        value = jnp.concatenate([value, other], axis=dim)
    flip = [sum(((p >> b) & 1) << (bits - 1 - b) for b in range(bits)) for p in range(size)]
    flipped_me = sum(((me >> b) & 1) << (bits - 1 - b) for b in range(bits))
    table = jnp.array(flip, jnp.int32)
    return value, jnp.bitwise_xor(table, me), jnp.bitwise_xor(table, flipped_me)


def in_order(value, holder, place, dim):
    size = holder.shape[0]
    shape = value.shape
    blocks = value.reshape(shape[:dim] + (size, shape[dim] // size) + shape[dim + 1 :])
    return jnp.take(blocks, place, axis=dim).reshape(shape)


def scatter_chunks(value, axis):
    size = lax.axis_size(axis)
    return value.reshape((size, value.shape[0] // size) + value.shape[1:])


def scatter_step(value, axis, bit):
    size = lax.axis_size(axis)
    mine = (lax.axis_index(axis) >> bit) & 1
    pairs = value.reshape((value.shape[0] // 2, 2) + value.shape[1:])
    keep = lax.dynamic_index_in_dim(pairs, mine, axis=1, keepdims=False)
    send = lax.dynamic_index_in_dim(pairs, 1 - mine, axis=1, keepdims=False)
    return keep + lax.ppermute(send, axis, [(i, i ^ (1 << bit)) for i in range(size)])


def paired_scatter(lead, follow, axis):
    size = lax.axis_size(axis)
    if size & (size - 1):
        return (
            lax.psum_scatter(lead, axis, scatter_dimension=0, tiled=True),
            lax.psum_scatter(follow, axis, scatter_dimension=0, tiled=True),
        )
    lead = scatter_chunks(lead, axis)
    follow = scatter_chunks(follow, axis)
    bit = 0
    while (1 << bit) < size:
        lead = scatter_step(lead, axis, bit)
        follow, _ = lax.optimization_barrier((follow, lead))
        follow = scatter_step(follow, axis, bit)
        bit += 1
    return lead[0], follow[0]


def shards(basis_values, aux_values, factors, frag_slot, dimer_pairs, counts, weights, metric_inv):
    highest = lax.Precision.HIGHEST
    basis_rows = basis_values[0]
    aux_block = aux_values[0]
    points = basis_rows.shape[0]
    naux = aux_block.shape[1]
    frag_basis = basis_rows.shape[1] // 2
    live_count = counts[0, 0]
    position = lax.iota(jnp.int32, points)
    live_weight = jnp.where(position < live_count, weights[0], jnp.zeros((), jnp.float32))
    gathered, slot_held, _ = xor_gather(factors, "dimer", 0)
    frag_ids = lax.iota(jnp.int32, frag_slot.shape[0])
    wanted = jnp.sum(
        jnp.where(frag_ids[None, :] == dimer_pairs[0][:, None], frag_slot[None, :], 0), axis=1
    )
    selector = (slot_held[None, :] == wanted[:, None]).astype(jnp.bfloat16)
    chosen = jnp.einsum(
        "as,srk->ark", selector, gathered, preferred_element_type=jnp.float32
    ).astype(jnp.bfloat16)
    dimer_factors = in_order(*xor_gather(chosen, "grid", 1), 1)
    nocc = dimer_factors.shape[2]
    empty = jnp.zeros((frag_basis, nocc), jnp.bfloat16)
    block_factors = jnp.concatenate(
        [
            jnp.concatenate([dimer_factors[0], empty], axis=1),
            jnp.concatenate([empty, dimer_factors[1]], axis=1),
        ],
        axis=0,
    )
    orbitals = jnp.dot(basis_rows, block_factors, preferred_element_type=jnp.float32)
    density = jnp.sum(orbitals * orbitals, axis=1) / (2.0 * nocc)
    exchange = -exchange_coeff * jnp.cbrt(density)
    weighted_density = live_weight * density
    high_rows, low_rows = split_rows(jnp.stack([weighted_density, live_weight]))
    projections = jnp.dot(
        jnp.concatenate([high_rows, low_rows]), aux_block, preferred_element_type=jnp.float32
    )
    sums_part = jnp.stack([jnp.sum(live_weight * exchange), jnp.sum(live_weight)])
    first_lane = lax.broadcasted_iota(jnp.int32, (2, 128), 1) == 0
    payload = jnp.concatenate(
        [projections[:2] + projections[2:], jnp.where(first_lane, sums_part[:, None], 0.0)], axis=1
    )
    totals = xor_sum(payload, "grid")
    fitted = totals[0, :naux]
    weight_projection = totals[1, :naux]
    exchange_total = totals[0, naux]
    weight_sum = totals[1, naux]
    coef_rows = jnp.sum(metric_inv[0] * fitted[None, :], axis=1)
    coefficients = in_order(*xor_gather(coef_rows, "grid", 0), 0)
    coulomb = jnp.sum(aux_block.astype(jnp.float32) * coefficients[None, :], axis=1)
    potential_total = jnp.dot(coefficients, weight_projection, precision=highest) + exchange_total
    average = potential_total / weight_sum
    potential = live_weight * (coulomb + exchange - average)
    weighted_basis = (basis_rows * potential[:, None]).astype(jnp.bfloat16)
    half_rows = frag_basis // lax.axis_size("grid")
    left_first = lax.slice_in_dim(weighted_basis, 0, half_rows * lax.axis_size("grid"), axis=1)
    left_second = lax.dynamic_slice_in_dim(
        weighted_basis, frag_basis, half_rows * lax.axis_size("grid"), 1
    )
    first_first = contract(left_first, basis_rows[:, :frag_basis])
    first_second = contract(left_first, basis_rows[:, frag_basis:])
    second_second = contract(left_second, basis_rows[:, frag_basis:])
    diagonal, own_cross = paired_scatter(
        jnp.stack([first_first, second_second], axis=1), first_second, "grid"
    )
    own_first = diagonal[:, 0]
    own_second = diagonal[:, 1]
    groups = lax.axis_size("dimer")
    me = lax.axis_index("dimer")
    zero = jnp.zeros((), jnp.float32)

    def piece(dest):
        return jnp.where(dimer_pairs[0, 0] == dest, own_first, zero) + jnp.where(
            dimer_pairs[0, 1] == dest, own_second, zero
        )

    frag_fock = piece(me)
    paired = groups & (groups - 1) == 0
    for shift in range(1, groups):
        if paired:
            dest, pairs = jnp.bitwise_xor(me, shift), [(i, i ^ shift) for i in range(groups)]
        else:
            dest, pairs = lax.rem(me + shift, groups), [(i, (i + shift) % groups) for i in range(groups)]
        frag_fock = frag_fock + lax.ppermute(piece(dest), "dimer", pairs)
    return (frag_fock[None], own_cross[None])


def solution(mesh):
    placed = (
        P("dimer", "grid", None),
        P("dimer", "grid", None),
        P("dimer", "grid", None),
        P(),
        P("dimer", None),
        P("dimer", "grid"),
        P("dimer", "grid"),
        P("dimer", "grid", None),
    )
    return jax.shard_map(
        shards,
        mesh=mesh,
        in_specs=placed,
        out_specs=(P("dimer", "grid", None), P("dimer", "grid", None)),
        check_vma=False,
    )
```
